128 devices in a mesh: panel: 16 (over z_hi, y, core), col: 8 (over z_lo, x).
Axes of the slice: x: 4, y: 4, z: 4 (z_hi: 2, z_lo: 2; z = z_hi * 2 + z_lo), core: 2. Of those that a mesh axis runs over, the one named last changes fastest.
Arguments:
- panel_rows: bfloat16 [32768, 512], P(('panel', 'col')), may hold values from -6 to 6
- diag_blocks: float32 [512, 512], replicated
- adjoint: bfloat16 [32768, 32768], P('panel', 'col')
- fill: int32 [128, 128], P('panel', 'col'), may hold values from 0 to 1, as said below
Outputs:
- grad_panel: float32 [32768, 512], P(('panel', 'col'))
- grad_diag: float32 [512, 512], replicated
The draws below stay inside these ranges and needn't reach their ends.
Inputs may be any that keep to these rules, and one draw needn't show every extreme that they name: fill is 1 on every diagonal block, fill equals its transpose, and adjoint equals its transpose.
All inputs are finite; a program needn't handle non-finite values.
Results may differ from the reference program's by a relative error of at most 0.004.
Values may be sent and summed in bfloat16 or wider, within the bound.
No kernel may reach another device: no remote copies, remote signals or barrier semaphores. Data moves between devices by JAX's collectives and lax.ppermute only.
A program may use at most 128 MiB of HBM per device.

```python
import jax
import jax.numpy as jnp
from jax import lax

B = 256
PW = 512
M = 32768


def draw_diag_blocks(key, part):
    first = jax.random.fold_in(key, 11)
    second = jax.random.fold_in(key, 12)
    amplitude = 2.0 / PW
    noise = jax.random.uniform(first, (PW, PW), jnp.float32, -1.0, 1.0)
    diag = jnp.exp(jax.random.uniform(second, (PW,), jnp.float32, jnp.log(2.5), jnp.log(4.0)))
    off = 0.5 * (noise + noise.T) * amplitude
    eye = (jnp.arange(PW)[:, None] == jnp.arange(PW)[None, :]).astype(jnp.float32)
    return (off * (1.0 - eye) + eye * diag[None, :]).astype(jnp.float32)


def draw_adjoint(key, part):
    first = jax.random.fold_in(key, 21)
    noise = jax.random.normal(first, (M, M), jnp.float32)
    return ((noise + noise.T) * 0.5 ** 0.5 * M ** (-0.5)).astype(jnp.bfloat16)


def draw_fill(key, part):
    first = jax.random.fold_in(key, 31)
    blocks = M // B
    marks = jax.random.randint(first, (blocks, blocks), 0, 4)
    both = jnp.minimum(marks, marks.T) > 0
    eye = jnp.arange(blocks)[:, None] == jnp.arange(blocks)[None, :]
    return jnp.where(eye | both, 1, 0).astype(jnp.int32)


def steps_of(rng, extent, shards, low, top_value):
    def one(dim, shards_of):
        heights = jax.random.uniform(jax.random.fold_in(jax.random.fold_in(rng, 6), dim), (shards_of,), jnp.float32, low / len(shards), top_value / len(shards))
        return jnp.repeat(jnp.exp(heights), extent[dim] // shards_of).reshape((-1,) + (1,) * (len(extent) - dim - 1))

    factor_of = one(*shards[0])
    for cut in shards[1:]:
        factor_of = factor_of * one(*cut)
    return factor_of


def centred(rng, shape, width, most, pieces=(), held_as=jnp.bfloat16):
    entries = jax.random.normal(rng, shape, jnp.float32) * width
    if len(pieces) > 0:
        entries = steps_of(rng, shape, pieces, -0.22, 0.18) * entries
    return jnp.clip(entries, min=-most, max=most).astype(held_as)


def setup_inputs(seed: int = 0) -> dict:
    seeds = jax.random.split(jax.random.key(seed), 5)
    return {
        "panel_rows": centred(seeds[0], (M, PW), 1.0, 6.0, ((0, 128),)),
        "diag_blocks": draw_diag_blocks(jax.random.fold_in(seeds[4], 71), 0),
        "adjoint": draw_adjoint(jax.random.fold_in(seeds[4], 71), 0),
        "fill": draw_fill(jax.random.fold_in(seeds[4], 71), 0),
    }


def factor_with_logdet(matrix):
    lower = jnp.linalg.cholesky(matrix)
    return (lower, 2.0 * jnp.sum(jnp.log(jnp.diagonal(lower))))

def reference(panel_rows, diag_blocks, adjoint, fill):
    lower = jnp.linalg.cholesky(diag_blocks)
    scaled = jax.scipy.linalg.solve_triangular(lower, panel_rows.astype(jnp.float32).T, lower=True).T.astype(jnp.bfloat16)
    blocks = fill.shape[0]

    def block_row(index):
        start = (index * B).astype(jnp.int32)
        rows = lax.dynamic_slice_in_dim(adjoint, start, B, 0)
        marks = lax.dynamic_slice_in_dim(fill, index.astype(jnp.int32), 1, 0)[0].astype(jnp.bfloat16)
        masked = (rows.reshape(B, blocks, B) * marks[None, :, None]).reshape(B, blocks * B)
        return jnp.dot(masked.astype(jnp.float32), scaled.astype(jnp.float32), preferred_element_type=jnp.float32)
    product = lax.map(block_row, jnp.arange(blocks, dtype=jnp.int32)).reshape(blocks * B, PW)
    grad_scaled = -product
    grad_panel = jax.scipy.linalg.solve_triangular(lower, grad_scaled.T, lower=True, trans=1).T
    grad_lower = -jnp.dot(grad_panel.T, scaled.astype(jnp.float32), precision=lax.Precision.HIGHEST)
    grad_lower = jnp.tril(grad_lower)
    outputs, pullback = jax.vjp(factor_with_logdet, diag_blocks)
    grad_diag = pullback((grad_lower, jnp.ones((), jnp.float32)))[0]
    return (grad_panel, grad_diag)
```

```python
import jax
import jax.numpy as jnp
from jax import lax
from jax.sharding import PartitionSpec as P

B = 256
F32 = jnp.float32
BF16 = jnp.bfloat16
HIGHEST = lax.Precision.HIGHEST


def shift(x, axis, n, s):
    return lax.ppermute(x, axis, [(i, (i + s) % n) for i in range(n)])


def gather_ring(x, axis, n, me):
    got = [x] + [shift(x, axis, n, s) for s in range(1, n)]
    held = jnp.stack([got[(-m) % n] for m in range(n)])
    return jnp.roll(held, me, axis=0).reshape((-1,) + x.shape[1:])


def scatter_sum(x, axis, n, me):
    rows = x.shape[0] // n
    acc = lax.dynamic_slice_in_dim(x, me * rows, rows, 0)
    for s in range(1, n):
        part = lax.dynamic_slice_in_dim(x, ((me + s) % n) * rows, rows, 0)
        acc = acc + shift(part, axis, n, s)
    return acc


def all_sum(x, n_col, n_pan, c, p):
    y = scatter_sum(x, "col", n_col, c)
    z = scatter_sum(y, "panel", n_pan, p)
    y = gather_ring(z, "panel", n_pan, p)
    return gather_ring(y, "col", n_col, c)


def split3(w):
    hi = lax.reduce_precision(w, exponent_bits=8, mantissa_bits=7)
    r = w - hi
    mid = lax.reduce_precision(r, exponent_bits=8, mantissa_bits=7)
    lo = r - mid
    return hi.astype(BF16), mid.astype(BF16), lo.astype(BF16)


def apply_split(x, parts):
    hi, mid, lo = parts
    d = lambda w: jnp.dot(x, w, preferred_element_type=F32)
    return d(hi) + (d(mid) + d(lo))


def shards(panel_rows, diag_blocks, adjoint, fill):
    n_col = lax.axis_size("col")
    n_pan = lax.axis_size("panel")
    c = lax.axis_index("col")
    p = lax.axis_index("panel")
    piece, width = panel_rows.shape

    flat = n_pan * n_col
    perm = [((dst % n_col) * n_pan + dst // n_col, dst) for dst in range(flat)]
    mine = lax.ppermute(panel_rows, ("panel", "col"), perm)
    col_rows = lax.all_gather(mine, "panel", axis=0, tiled=True)

    lower = jnp.linalg.cholesky(diag_blocks)
    linv = jax.scipy.linalg.solve_triangular(lower, jnp.eye(width, dtype=F32), lower=True)
    parts = split3(linv.T)
    scaled_cols = apply_split(col_rows, parts).astype(BF16)
    scaled = apply_split(panel_rows, parts).astype(BF16)

    marks = fill.astype(BF16)
    col_blocks = fill.shape[1]
    per = piece // B

    def product(k):
        rows = lax.dynamic_slice_in_dim(adjoint, k * piece, piece, 0)
        m = lax.dynamic_slice_in_dim(marks, k * per, per, 0)
        masked = (rows.reshape(per, B, col_blocks, B) * m[:, None, :, None]).reshape(piece, -1)
        return jnp.dot(masked, scaled_cols, preferred_element_type=F32)

    total = product(c)
    for s in range(1, n_col):
        total = total + shift(product((c + s) % n_col), "col", n_col, s)
    grad_scaled = -total
    grad_panel = jnp.dot(grad_scaled, linv, precision=HIGHEST)
    partial_lower = -jnp.dot(grad_panel.T, scaled.astype(F32), precision=HIGHEST)
    grad_lower = jnp.tril(all_sum(partial_lower, n_col, n_pan, c, p))

    diag = jnp.diagonal(lower)
    eye = jnp.eye(width, dtype=F32)
    bar = grad_lower + eye * (2.0 / diag)[None, :]
    inner = jnp.tril(jnp.dot(lower.T, bar, precision=HIGHEST)) * (1.0 - 0.5 * eye)
    sigma = jnp.dot(jnp.dot(linv.T, inner, precision=HIGHEST), linv, precision=HIGHEST)
    grad_diag = 0.5 * (sigma + sigma.T)
    return (grad_panel, grad_diag)


def solution(mesh):
    in_specs = (P(("panel", "col"), None), P(), P("panel", "col"), P("panel", "col"))
    out_specs = (P(("panel", "col"), None), P())
    return jax.shard_map(shards, mesh=mesh, in_specs=in_specs, out_specs=out_specs, check_vma=False)
```

```python
import jax
import jax.numpy as jnp
from jax import lax
from jax.sharding import PartitionSpec as P

B = 256
F32 = jnp.float32
BF16 = jnp.bfloat16
HIGHEST = lax.Precision.HIGHEST


def shift(x, axis, n, s):
    return lax.ppermute(x, axis, [(i, (i + s) % n) for i in range(n)])


def gather_ring(x, axis, n, me):
    got = [x] + [shift(x, axis, n, s) for s in range(1, n)]
    held = jnp.stack([got[(-m) % n] for m in range(n)])
    return jnp.roll(held, me, axis=0).reshape((-1,) + x.shape[1:])


def scatter_sum(x, axis, n, me):
    rows = x.shape[0] // n
    acc = lax.dynamic_slice_in_dim(x, me * rows, rows, 0)
    for s in range(1, n):
        part = lax.dynamic_slice_in_dim(x, ((me + s) % n) * rows, rows, 0)
        acc = acc + shift(part, axis, n, s)
    return acc


def all_sum(x, n_col, n_pan, c, p):
    y = scatter_sum(x, "col", n_col, c)
    z = scatter_sum(y, "panel", n_pan, p)
    y = gather_ring(z, "panel", n_pan, p)
    return gather_ring(y, "col", n_col, c)


def split3(w):
    hi = lax.reduce_precision(w, exponent_bits=8, mantissa_bits=7)
    r = w - hi
    mid = lax.reduce_precision(r, exponent_bits=8, mantissa_bits=7)
    lo = r - mid
    return hi.astype(BF16), mid.astype(BF16), lo.astype(BF16)


def apply_split(x, parts):
    hi, mid, lo = parts
    d = lambda w: jnp.dot(x, w, preferred_element_type=F32)
    return d(hi) + (d(mid) + d(lo))


def halving_sum(x, stages):
    bits = []
    for axis, n, me, b in stages:
        bit = (me // b) % 2
        pairs = [(i, i ^ b) for i in range(n)]
        h = x.shape[0] // 2
        keep = lax.dynamic_slice_in_dim(x, bit * h, h, 0)
        send = lax.dynamic_slice_in_dim(x, (1 - bit) * h, h, 0)
        x = keep + lax.ppermute(send, axis, pairs)
        bits.append((axis, pairs, bit))
    for axis, pairs, bit in reversed(bits):
        other = lax.ppermute(x, axis, pairs)
        x = jnp.where(bit == 0, jnp.concatenate([x, other]), jnp.concatenate([other, x]))
    return x


def shards(panel_rows, diag_blocks, adjoint, fill):
    n_col = lax.axis_size("col")
    n_pan = lax.axis_size("panel")
    c = lax.axis_index("col")
    p = lax.axis_index("panel")
    piece, width = panel_rows.shape

    flat = n_pan * n_col
    got = []
    for t in range(n_pan):
        perm = [((dst % n_col) * n_pan + (dst // n_col + t) % n_pan, dst) for dst in range(flat)]
        got.append(lax.ppermute(panel_rows, ("panel", "col"), perm))
    col_rows = jnp.roll(jnp.stack(got), p, axis=0).reshape(-1, width)

    marks = fill.astype(BF16)
    col_blocks = fill.shape[1]
    per = piece // B

    def product(k):
        rows = lax.dynamic_slice_in_dim(adjoint, k * piece, piece, 0)
        m = lax.dynamic_slice_in_dim(marks, k * per, per, 0)
        masked = (rows.reshape(per, B, col_blocks, B) * m[:, None, :, None]).reshape(piece, -1)
        return jnp.dot(masked, col_rows, preferred_element_type=F32)

    total = product(c)
    for s in range(1, n_col):
        total = total + shift(product((c + s) % n_col), "col", n_col, s)
    moment = jnp.dot(total.T, panel_rows.astype(F32), precision=HIGHEST)
    stages = [("panel", n_pan, p, 1)]
    stages += [("col", n_col, c, 1 << k) for k in range(n_col.bit_length() - 1)]
    stages += [("panel", n_pan, p, 1 << k) for k in range(1, n_pan.bit_length() - 1)]
    moment = halving_sum(moment, stages)

    lower = jnp.linalg.cholesky(diag_blocks)
    linv = jax.scipy.linalg.solve_triangular(lower, jnp.eye(width, dtype=F32), lower=True)
    minv = jnp.dot(linv.T, linv, precision=HIGHEST)
    grad_panel = -jnp.dot(total, minv, precision=HIGHEST)
    grad_lower = jnp.tril(jnp.dot(jnp.dot(minv, moment, precision=HIGHEST), linv.T, precision=HIGHEST))

    diag = jnp.diagonal(lower)
    eye = jnp.eye(width, dtype=F32)
    bar = grad_lower + eye * (2.0 / diag)[None, :]
    inner = jnp.tril(jnp.dot(lower.T, bar, precision=HIGHEST)) * (1.0 - 0.5 * eye)
    sigma = jnp.dot(jnp.dot(linv.T, inner, precision=HIGHEST), linv, precision=HIGHEST)
    grad_diag = 0.5 * (sigma + sigma.T)
    return (grad_panel, grad_diag)


def solution(mesh):
    in_specs = (P(("panel", "col"), None), P(), P("panel", "col"), P("panel", "col"))
    out_specs = (P(("panel", "col"), None), P())
    return jax.shard_map(shards, mesh=mesh, in_specs=in_specs, out_specs=out_specs, check_vma=False)
```

```python
import jax
import jax.numpy as jnp
from jax import lax
from jax.sharding import PartitionSpec as P

B = 256
F32 = jnp.float32
BF16 = jnp.bfloat16
HIGHEST = lax.Precision.HIGHEST


def shift(x, axis, n, s):
    return lax.ppermute(x, axis, [(i, (i + s) % n) for i in range(n)])


def gather_ring(x, axis, n, me):
    got = [x] + [shift(x, axis, n, s) for s in range(1, n)]
    held = jnp.stack([got[(-m) % n] for m in range(n)])
    return jnp.roll(held, me, axis=0).reshape((-1,) + x.shape[1:])


def scatter_sum(x, axis, n, me):
    rows = x.shape[0] // n
    acc = lax.dynamic_slice_in_dim(x, me * rows, rows, 0)
    for s in range(1, n):
        part = lax.dynamic_slice_in_dim(x, ((me + s) % n) * rows, rows, 0)
        acc = acc + shift(part, axis, n, s)
    return acc


def all_sum(x, n_col, n_pan, c, p):
    y = scatter_sum(x, "col", n_col, c)
    z = scatter_sum(y, "panel", n_pan, p)
    y = gather_ring(z, "panel", n_pan, p)
    return gather_ring(y, "col", n_col, c)


def split3(w):
    hi = lax.reduce_precision(w, exponent_bits=8, mantissa_bits=7)
    r = w - hi
    mid = lax.reduce_precision(r, exponent_bits=8, mantissa_bits=7)
    lo = r - mid
    return hi.astype(BF16), mid.astype(BF16), lo.astype(BF16)


def apply_split(x, parts):
    hi, mid, lo = parts
    d = lambda w: jnp.dot(x, w, preferred_element_type=F32)
    return d(hi) + (d(mid) + d(lo))


def halving_sum(x, stages):
    bits = []
    for axis, n, me, b in stages:
        bit = (me // b) % 2
        pairs = [(i, i ^ b) for i in range(n)]
        h = x.shape[0] // 2
        keep = lax.dynamic_slice_in_dim(x, bit * h, h, 0)
        send = lax.dynamic_slice_in_dim(x, (1 - bit) * h, h, 0)
        x = keep + lax.ppermute(send, axis, pairs)
        bits.append((axis, pairs, bit))
    for axis, pairs, bit in reversed(bits):
        other = lax.ppermute(x, axis, pairs)
        x = jnp.where(bit == 0, jnp.concatenate([x, other]), jnp.concatenate([other, x]))
    return x


def shards(panel_rows, diag_blocks, adjoint, fill):
    n_col = lax.axis_size("col")
    n_pan = lax.axis_size("panel")
    c = lax.axis_index("col")
    p = lax.axis_index("panel")
    piece, width = panel_rows.shape

    flat = n_pan * n_col
    perm = [((dst % n_col) * n_pan + dst // n_col, dst) for dst in range(flat)]
    mine = lax.ppermute(panel_rows, ("panel", "col"), perm)
    col_rows = lax.all_gather(mine, "panel", axis=0, tiled=True)

    marks = fill.astype(BF16)
    col_blocks = fill.shape[1]
    per = piece // B

    def product(k):
        rows = lax.dynamic_slice_in_dim(adjoint, k * piece, piece, 0)
        m = lax.dynamic_slice_in_dim(marks, k * per, per, 0)
        masked = (rows.reshape(per, B, col_blocks, B) * m[:, None, :, None]).reshape(piece, -1)
        return jnp.dot(masked, col_rows, preferred_element_type=F32)

    total = product(c)
    for s in range(1, n_col):
        total = total + shift(product((c + s) % n_col), "col", n_col, s)
    moment = jnp.dot(total.T, panel_rows.astype(F32), precision=HIGHEST)
    stages = [("panel", n_pan, p, 1)]
    stages += [("col", n_col, c, 1 << k) for k in range(n_col.bit_length() - 1)]
    stages += [("panel", n_pan, p, 1 << k) for k in range(1, n_pan.bit_length() - 1)]
    moment = halving_sum(moment, stages)

    lower = jnp.linalg.cholesky(diag_blocks)
    linv = jax.scipy.linalg.solve_triangular(lower, jnp.eye(width, dtype=F32), lower=True)
    minv = jnp.dot(linv.T, linv, precision=HIGHEST)
    grad_panel = -jnp.dot(total, minv, precision=HIGHEST)
    grad_lower = jnp.tril(jnp.dot(jnp.dot(minv, moment, precision=HIGHEST), linv.T, precision=HIGHEST))

    diag = jnp.diagonal(lower)
    eye = jnp.eye(width, dtype=F32)
    bar = grad_lower + eye * (2.0 / diag)[None, :]
    inner = jnp.tril(jnp.dot(lower.T, bar, precision=HIGHEST)) * (1.0 - 0.5 * eye)
    sigma = jnp.dot(jnp.dot(linv.T, inner, precision=HIGHEST), linv, precision=HIGHEST)
    grad_diag = 0.5 * (sigma + sigma.T)
    return (grad_panel, grad_diag)


def solution(mesh):
    in_specs = (P(("panel", "col"), None), P(), P("panel", "col"), P("panel", "col"))
    out_specs = (P(("panel", "col"), None), P())
    return jax.shard_map(shards, mesh=mesh, in_specs=in_specs, out_specs=out_specs, check_vma=False)
```

```python
import jax
import jax.numpy as jnp
from jax import lax
from jax.sharding import PartitionSpec as P

B = 256
F32 = jnp.float32
BF16 = jnp.bfloat16
HIGHEST = lax.Precision.HIGHEST


def shift(x, axis, n, s):
    return lax.ppermute(x, axis, [(i, (i + s) % n) for i in range(n)])


def gather_ring(x, axis, n, me):
    got = [x] + [shift(x, axis, n, s) for s in range(1, n)]
    held = jnp.stack([got[(-m) % n] for m in range(n)])
    return jnp.roll(held, me, axis=0).reshape((-1,) + x.shape[1:])


def scatter_sum(x, axis, n, me):
    rows = x.shape[0] // n
    acc = lax.dynamic_slice_in_dim(x, me * rows, rows, 0)
    for s in range(1, n):
        part = lax.dynamic_slice_in_dim(x, ((me + s) % n) * rows, rows, 0)
        acc = acc + shift(part, axis, n, s)
    return acc


def all_sum(x, n_col, n_pan, c, p):
    y = scatter_sum(x, "col", n_col, c)
    z = scatter_sum(y, "panel", n_pan, p)
    y = gather_ring(z, "panel", n_pan, p)
    return gather_ring(y, "col", n_col, c)


def split3(w):
    hi = lax.reduce_precision(w, exponent_bits=8, mantissa_bits=7)
    r = w - hi
    mid = lax.reduce_precision(r, exponent_bits=8, mantissa_bits=7)
    lo = r - mid
    return hi.astype(BF16), mid.astype(BF16), lo.astype(BF16)


def apply_split(x, parts):
    hi, mid, lo = parts
    d = lambda w: jnp.dot(x, w, preferred_element_type=F32)
    return d(hi) + (d(mid) + d(lo))


def halving_sum(x, stages):
    bits = []
    for axis, n, me, b in stages:
        bit = (me // b) % 2
        pairs = [(i, i ^ b) for i in range(n)]
        h = x.shape[0] // 2
        keep = lax.dynamic_slice_in_dim(x, bit * h, h, 0)
        send = lax.dynamic_slice_in_dim(x, (1 - bit) * h, h, 0)
        x = keep + lax.ppermute(send, axis, pairs)
        bits.append((axis, pairs, bit))
    for axis, pairs, bit in reversed(bits):
        other = lax.ppermute(x, axis, pairs)
        x = jnp.where(bit == 0, jnp.concatenate([x, other]), jnp.concatenate([other, x]))
    return x


def factor_and_inverse(matrix, b=128):
    n = matrix.shape[0]
    nb = n // b
    a = 0.5 * (matrix + matrix.T)
    cols = []
    invs = []
    for j in range(nb):
        lo, hi = j * b, (j + 1) * b
        below = a[lo:, lo:hi]
        if j > 0:
            left = jnp.concatenate([cl[lo - k * b:] for k, cl in enumerate(cols)], axis=1)
            below = below - jnp.dot(left, left[:b].T, precision=HIGHEST)
        ljj = jnp.linalg.cholesky(below[:b])
        ijj = jax.scipy.linalg.solve_triangular(ljj, jnp.eye(b, dtype=F32), lower=True)
        rest = jnp.dot(below[b:], ijj.T, precision=HIGHEST)
        cols.append(jnp.concatenate([jnp.tril(ljj), rest], axis=0))
        invs.append(ijj)
    lower = jnp.concatenate(
        [jnp.pad(cl, ((k * b, 0), (0, 0))) for k, cl in enumerate(cols)], axis=1)
    linv = invs[0]
    for i in range(1, nb):
        lo, hi = i * b, (i + 1) * b
        row = -jnp.dot(invs[i], jnp.dot(lower[lo:hi, :lo], linv, precision=HIGHEST), precision=HIGHEST)
        top = jnp.pad(linv, ((0, 0), (0, b)))
        bottom = jnp.concatenate([row, invs[i]], axis=1)
        linv = jnp.concatenate([top, bottom], axis=0)
    return lower, linv


def shards(panel_rows, diag_blocks, adjoint, fill):
    n_col = lax.axis_size("col")
    n_pan = lax.axis_size("panel")
    c = lax.axis_index("col")
    p = lax.axis_index("panel")
    piece, width = panel_rows.shape

    flat = n_pan * n_col
    perm = [((dst % n_col) * n_pan + dst // n_col, dst) for dst in range(flat)]
    mine = lax.ppermute(panel_rows, ("panel", "col"), perm)
    col_rows = lax.all_gather(mine, "panel", axis=0, tiled=True)

    marks = fill.astype(BF16)
    col_blocks = fill.shape[1]
    per = piece // B

    def product(k):
        rows = lax.dynamic_slice_in_dim(adjoint, k * piece, piece, 0)
        m = lax.dynamic_slice_in_dim(marks, k * per, per, 0)
        masked = (rows.reshape(per, B, col_blocks, B) * m[:, None, :, None]).reshape(piece, -1)
        return jnp.dot(masked, col_rows, preferred_element_type=F32)

    total = product(c)
    for s in range(1, n_col):
        total = total + shift(product((c + s) % n_col), "col", n_col, s)
    moment = jnp.dot(total.T, panel_rows.astype(F32), precision=HIGHEST)
    stages = [("panel", n_pan, p, 1)]
    stages += [("col", n_col, c, 1 << k) for k in range(n_col.bit_length() - 1)]
    stages += [("panel", n_pan, p, 1 << k) for k in range(1, n_pan.bit_length() - 1)]
    moment = halving_sum(moment, stages)

    lower, linv = factor_and_inverse(diag_blocks)
    minv = jnp.dot(linv.T, linv, precision=HIGHEST)
    grad_panel = -jnp.dot(total, minv, precision=HIGHEST)
    grad_lower = jnp.tril(jnp.dot(jnp.dot(minv, moment, precision=HIGHEST), linv.T, precision=HIGHEST))

    diag = jnp.diagonal(lower)
    eye = jnp.eye(width, dtype=F32)
    bar = grad_lower + eye * (2.0 / diag)[None, :]
    inner = jnp.tril(jnp.dot(lower.T, bar, precision=HIGHEST)) * (1.0 - 0.5 * eye)
    sigma = jnp.dot(jnp.dot(linv.T, inner, precision=HIGHEST), linv, precision=HIGHEST)
    grad_diag = 0.5 * (sigma + sigma.T)
    return (grad_panel, grad_diag)


def solution(mesh):
    in_specs = (P(("panel", "col"), None), P(), P("panel", "col"), P("panel", "col"))
    out_specs = (P(("panel", "col"), None), P())
    return jax.shard_map(shards, mesh=mesh, in_specs=in_specs, out_specs=out_specs, check_vma=False)
```

```python
import jax
import jax.numpy as jnp
from jax import lax
from jax.sharding import PartitionSpec as P

B = 256
F32 = jnp.float32
BF16 = jnp.bfloat16
HIGHEST = lax.Precision.HIGHEST


def shift(x, axis, n, s):
    return lax.ppermute(x, axis, [(i, (i + s) % n) for i in range(n)])


def gather_ring(x, axis, n, me):
    got = [x] + [shift(x, axis, n, s) for s in range(1, n)]
    held = jnp.stack([got[(-m) % n] for m in range(n)])
    return jnp.roll(held, me, axis=0).reshape((-1,) + x.shape[1:])


def scatter_sum(x, axis, n, me):
    rows = x.shape[0] // n
    acc = lax.dynamic_slice_in_dim(x, me * rows, rows, 0)
    for s in range(1, n):
        part = lax.dynamic_slice_in_dim(x, ((me + s) % n) * rows, rows, 0)
        acc = acc + shift(part, axis, n, s)
    return acc


def all_sum(x, n_col, n_pan, c, p):
    y = scatter_sum(x, "col", n_col, c)
    z = scatter_sum(y, "panel", n_pan, p)
    y = gather_ring(z, "panel", n_pan, p)
    return gather_ring(y, "col", n_col, c)


def split3(w):
    hi = lax.reduce_precision(w, exponent_bits=8, mantissa_bits=7)
    r = w - hi
    mid = lax.reduce_precision(r, exponent_bits=8, mantissa_bits=7)
    lo = r - mid
    return hi.astype(BF16), mid.astype(BF16), lo.astype(BF16)


def apply_split(x, parts):
    hi, mid, lo = parts
    d = lambda w: jnp.dot(x, w, preferred_element_type=F32)
    return d(hi) + (d(mid) + d(lo))


def halving_sum(x, stages):
    bits = []
    for axis, n, me, b in stages:
        bit = (me // b) % 2
        pairs = [(i, i ^ b) for i in range(n)]
        h = x.shape[0] // 2
        keep = lax.dynamic_slice_in_dim(x, bit * h, h, 0)
        send = lax.dynamic_slice_in_dim(x, (1 - bit) * h, h, 0)
        x = keep + lax.ppermute(send, axis, pairs)
        bits.append((axis, pairs, bit))
    for axis, pairs, bit in reversed(bits):
        other = lax.ppermute(x, axis, pairs)
        x = jnp.where(bit == 0, jnp.concatenate([x, other]), jnp.concatenate([other, x]))
    return x


def factor_and_inverse(matrix, b=128):
    n = matrix.shape[0]
    nb = n // b
    a = 0.5 * (matrix + matrix.T)
    cols = []
    invs = []
    for j in range(nb):
        lo, hi = j * b, (j + 1) * b
        below = a[lo:, lo:hi]
        if j > 0:
            left = jnp.concatenate([cl[lo - k * b:] for k, cl in enumerate(cols)], axis=1)
            below = below - jnp.dot(left, left[:b].T, precision=HIGHEST)
        ljj = jnp.linalg.cholesky(below[:b])
        ijj = jax.scipy.linalg.solve_triangular(ljj, jnp.eye(b, dtype=F32), lower=True)
        rest = jnp.dot(below[b:], ijj.T, precision=HIGHEST)
        cols.append(jnp.concatenate([jnp.tril(ljj), rest], axis=0))
        invs.append(ijj)
    lower = jnp.concatenate(
        [jnp.pad(cl, ((k * b, 0), (0, 0))) for k, cl in enumerate(cols)], axis=1)
    linv = invs[0]
    for i in range(1, nb):
        lo, hi = i * b, (i + 1) * b
        row = -jnp.dot(invs[i], jnp.dot(lower[lo:hi, :lo], linv, precision=HIGHEST), precision=HIGHEST)
        top = jnp.pad(linv, ((0, 0), (0, b)))
        bottom = jnp.concatenate([row, invs[i]], axis=1)
        linv = jnp.concatenate([top, bottom], axis=0)
    return lower, linv


def shards(panel_rows, diag_blocks, adjoint, fill):
    n_col = lax.axis_size("col")
    n_pan = lax.axis_size("panel")
    c = lax.axis_index("col")
    p = lax.axis_index("panel")
    piece, width = panel_rows.shape

    flat = n_pan * n_col
    perm = [((dst % n_col) * n_pan + dst // n_col, dst) for dst in range(flat)]
    mine = lax.ppermute(panel_rows, ("panel", "col"), perm)
    col_rows = lax.all_gather(mine, "panel", axis=0, tiled=True)

    marks = fill.astype(BF16)
    col_blocks = fill.shape[1]
    per = piece // B

    def product(k):
        rows = lax.dynamic_slice_in_dim(adjoint, k * piece, piece, 0)
        m = lax.dynamic_slice_in_dim(marks, k * per, per, 0)
        masked = (rows.reshape(per, B, col_blocks, B) * m[:, None, :, None]).reshape(piece, -1)
        return jnp.dot(masked, col_rows, preferred_element_type=F32)

    def moment_of(part, k):
        rows = lax.dynamic_slice_in_dim(block_rows, k * piece, piece, 0)
        hi = lax.reduce_precision(part, exponent_bits=8, mantissa_bits=7)
        lo = part - hi
        d = lambda w: lax.dot_general(w.astype(BF16), rows, (((0,), (0,)), ((), ())),
                                      preferred_element_type=F32)
        return d(hi) + d(lo)

    block_rows = lax.all_gather(panel_rows, "col", axis=0, tiled=True)
    total = product(c)
    moment = moment_of(total, c)
    for s in range(1, n_col):
        k = (c + s) % n_col
        part = product(k)
        moment = moment + moment_of(part, k)
        total = total + shift(part, "col", n_col, s)
    stages = [("panel", n_pan, p, 1)]
    stages += [("col", n_col, c, 1 << k) for k in range(n_col.bit_length() - 1)]
    stages += [("panel", n_pan, p, 1 << k) for k in range(1, n_pan.bit_length() - 1)]
    moment = halving_sum(moment, stages)

    lower, linv = factor_and_inverse(diag_blocks)
    minv = jnp.dot(linv.T, linv, precision=HIGHEST)
    grad_panel = -jnp.dot(total, minv, precision=HIGHEST)
    grad_lower = jnp.tril(jnp.dot(jnp.dot(minv, moment, precision=HIGHEST), linv.T, precision=HIGHEST))

    diag = jnp.diagonal(lower)
    eye = jnp.eye(width, dtype=F32)
    bar = grad_lower + eye * (2.0 / diag)[None, :]
    inner = jnp.tril(jnp.dot(lower.T, bar, precision=HIGHEST)) * (1.0 - 0.5 * eye)
    sigma = jnp.dot(jnp.dot(linv.T, inner, precision=HIGHEST), linv, precision=HIGHEST)
    grad_diag = 0.5 * (sigma + sigma.T)
    return (grad_panel, grad_diag)


def solution(mesh):
    in_specs = (P(("panel", "col"), None), P(), P("panel", "col"), P("panel", "col"))
    out_specs = (P(("panel", "col"), None), P())
    return jax.shard_map(shards, mesh=mesh, in_specs=in_specs, out_specs=out_specs, check_vma=False)
```

```python
import jax
import jax.numpy as jnp
from jax import lax
from jax.sharding import PartitionSpec as P

B = 256
F32 = jnp.float32
BF16 = jnp.bfloat16
HIGHEST = lax.Precision.HIGHEST


def shift(x, axis, n, s):
    return lax.ppermute(x, axis, [(i, (i + s) % n) for i in range(n)])


def gather_ring(x, axis, n, me):
    got = [x] + [shift(x, axis, n, s) for s in range(1, n)]
    held = jnp.stack([got[(-m) % n] for m in range(n)])
    return jnp.roll(held, me, axis=0).reshape((-1,) + x.shape[1:])


def scatter_sum(x, axis, n, me):
    rows = x.shape[0] // n
    acc = lax.dynamic_slice_in_dim(x, me * rows, rows, 0)
    for s in range(1, n):
        part = lax.dynamic_slice_in_dim(x, ((me + s) % n) * rows, rows, 0)
        acc = acc + shift(part, axis, n, s)
    return acc


def all_sum(x, n_col, n_pan, c, p):
    y = scatter_sum(x, "col", n_col, c)
    z = scatter_sum(y, "panel", n_pan, p)
    y = gather_ring(z, "panel", n_pan, p)
    return gather_ring(y, "col", n_col, c)


def split3(w):
    hi = lax.reduce_precision(w, exponent_bits=8, mantissa_bits=7)
    r = w - hi
    mid = lax.reduce_precision(r, exponent_bits=8, mantissa_bits=7)
    lo = r - mid
    return hi.astype(BF16), mid.astype(BF16), lo.astype(BF16)


def apply_split(x, parts):
    hi, mid, lo = parts
    d = lambda w: jnp.dot(x, w, preferred_element_type=F32)
    return d(hi) + (d(mid) + d(lo))


def halving_sum(x, stages):
    bits = []
    for axis, n, me, b in stages:
        bit = (me // b) % 2
        pairs = [(i, i ^ b) for i in range(n)]
        h = x.shape[0] // 2
        keep = lax.dynamic_slice_in_dim(x, bit * h, h, 0)
        send = lax.dynamic_slice_in_dim(x, (1 - bit) * h, h, 0)
        x = keep + lax.ppermute(send, axis, pairs)
        bits.append((axis, pairs, bit))
    for axis, pairs, bit in reversed(bits):
        other = lax.ppermute(x, axis, pairs)
        x = jnp.where(bit == 0, jnp.concatenate([x, other]), jnp.concatenate([other, x]))
    return x


def factor_and_inverse(matrix, anchor, sync_after, b=128):
    n = matrix.shape[0]
    nb = n // b
    a = 0.5 * (matrix + matrix.T)
    cols = []
    invs = []
    for j in range(nb):
        lo, hi = j * b, (j + 1) * b
        below = a[lo:, lo:hi]
        if j > 0:
            left = jnp.concatenate([cl[lo - k * b:] for k, cl in enumerate(cols)], axis=1)
            below = below - jnp.dot(left, left[:b].T, precision=HIGHEST)
        ljj = jnp.linalg.cholesky(below[:b])
        ijj = jax.scipy.linalg.solve_triangular(ljj, jnp.eye(b, dtype=F32), lower=True)
        rest = jnp.dot(below[b:], ijj.T, precision=HIGHEST)
        cols.append(jnp.concatenate([jnp.tril(ljj), rest], axis=0))
        invs.append(ijj)
        if j == sync_after:
            (cols, invs), _ = lax.optimization_barrier(((cols, invs), anchor))
    lower = jnp.concatenate(
        [jnp.pad(cl, ((k * b, 0), (0, 0))) for k, cl in enumerate(cols)], axis=1)
    linv = invs[0]
    for i in range(1, nb):
        lo, hi = i * b, (i + 1) * b
        row = -jnp.dot(invs[i], jnp.dot(lower[lo:hi, :lo], linv, precision=HIGHEST), precision=HIGHEST)
        top = jnp.pad(linv, ((0, 0), (0, b)))
        bottom = jnp.concatenate([row, invs[i]], axis=1)
        linv = jnp.concatenate([top, bottom], axis=0)
    return lower, linv


def shards(panel_rows, diag_blocks, adjoint, fill):
    n_col = lax.axis_size("col")
    n_pan = lax.axis_size("panel")
    c = lax.axis_index("col")
    p = lax.axis_index("panel")
    piece, width = panel_rows.shape

    flat = n_pan * n_col
    perm = [((dst % n_col) * n_pan + dst // n_col, dst) for dst in range(flat)]
    mine = lax.ppermute(panel_rows, ("panel", "col"), perm)
    col_rows = lax.all_gather(mine, "panel", axis=0, tiled=True)

    marks = fill.astype(BF16)
    col_blocks = fill.shape[1]
    per = piece // B

    def product(k):
        rows = lax.dynamic_slice_in_dim(adjoint, k * piece, piece, 0)
        m = lax.dynamic_slice_in_dim(marks, k * per, per, 0)
        masked = (rows.reshape(per, B, col_blocks, B) * m[:, None, :, None]).reshape(piece, -1)
        return jnp.dot(masked, col_rows, preferred_element_type=F32)

    parts = [product((c + s) % n_col) for s in range(n_col)]
    total = parts[0]
    for s in range(1, n_col):
        total = total + shift(parts[s], "col", n_col, s)
    moment = jnp.dot(total.T, panel_rows.astype(F32), precision=HIGHEST)
    stages = [("panel", n_pan, p, 1)]
    stages += [("col", n_col, c, 1 << k) for k in range(n_col.bit_length() - 1)]
    stages += [("panel", n_pan, p, 1 << k) for k in range(1, n_pan.bit_length() - 1)]
    moment = halving_sum(moment, stages)

    lower, linv = factor_and_inverse(diag_blocks, parts, 1)
    minv = jnp.dot(linv.T, linv, precision=HIGHEST)
    grad_panel = -jnp.dot(total, minv, precision=HIGHEST)
    grad_lower = jnp.tril(jnp.dot(jnp.dot(minv, moment, precision=HIGHEST), linv.T, precision=HIGHEST))

    diag = jnp.diagonal(lower)
    eye = jnp.eye(width, dtype=F32)
    bar = grad_lower + eye * (2.0 / diag)[None, :]
    inner = jnp.tril(jnp.dot(lower.T, bar, precision=HIGHEST)) * (1.0 - 0.5 * eye)
    sigma = jnp.dot(jnp.dot(linv.T, inner, precision=HIGHEST), linv, precision=HIGHEST)
    grad_diag = 0.5 * (sigma + sigma.T)
    return (grad_panel, grad_diag)


def solution(mesh):
    in_specs = (P(("panel", "col"), None), P(), P("panel", "col"), P("panel", "col"))
    out_specs = (P(("panel", "col"), None), P())
    return jax.shard_map(shards, mesh=mesh, in_specs=in_specs, out_specs=out_specs, check_vma=False)
```

```python
import jax
import jax.numpy as jnp
from jax import lax
from jax.sharding import PartitionSpec as P

B = 256
F32 = jnp.float32
BF16 = jnp.bfloat16
HIGHEST = lax.Precision.HIGHEST


def shift(x, axis, n, s):
    return lax.ppermute(x, axis, [(i, (i + s) % n) for i in range(n)])


def gather_ring(x, axis, n, me):
    got = [x] + [shift(x, axis, n, s) for s in range(1, n)]
    held = jnp.stack([got[(-m) % n] for m in range(n)])
    return jnp.roll(held, me, axis=0).reshape((-1,) + x.shape[1:])


def scatter_sum(x, axis, n, me):
    rows = x.shape[0] // n
    acc = lax.dynamic_slice_in_dim(x, me * rows, rows, 0)
    for s in range(1, n):
        part = lax.dynamic_slice_in_dim(x, ((me + s) % n) * rows, rows, 0)
        acc = acc + shift(part, axis, n, s)
    return acc


def all_sum(x, n_col, n_pan, c, p):
    y = scatter_sum(x, "col", n_col, c)
    z = scatter_sum(y, "panel", n_pan, p)
    y = gather_ring(z, "panel", n_pan, p)
    return gather_ring(y, "col", n_col, c)


def split3(w):
    hi = lax.reduce_precision(w, exponent_bits=8, mantissa_bits=7)
    r = w - hi
    mid = lax.reduce_precision(r, exponent_bits=8, mantissa_bits=7)
    lo = r - mid
    return hi.astype(BF16), mid.astype(BF16), lo.astype(BF16)


def apply_split(x, parts):
    hi, mid, lo = parts
    d = lambda w: jnp.dot(x, w, preferred_element_type=F32)
    return d(hi) + (d(mid) + d(lo))


def halving_sum(x, stages):
    bits = []
    for axis, n, me, b in stages:
        bit = (me // b) % 2
        pairs = [(i, i ^ b) for i in range(n)]
        h = x.shape[0] // 2
        keep = lax.dynamic_slice_in_dim(x, bit * h, h, 0)
        send = lax.dynamic_slice_in_dim(x, (1 - bit) * h, h, 0)
        x = keep + lax.ppermute(send, axis, pairs)
        bits.append((axis, pairs, bit))
    for axis, pairs, bit in reversed(bits):
        other = lax.ppermute(x, axis, pairs)
        x = jnp.where(bit == 0, jnp.concatenate([x, other]), jnp.concatenate([other, x]))
    return x


def factor_and_inverse(matrix, anchor, sync_after, b=128):
    n = matrix.shape[0]
    nb = n // b
    a = 0.5 * (matrix + matrix.T)
    cols = []
    invs = []
    for j in range(nb):
        lo, hi = j * b, (j + 1) * b
        below = a[lo:, lo:hi]
        if j > 0:
            left = jnp.concatenate([cl[lo - k * b:] for k, cl in enumerate(cols)], axis=1)
            below = below - jnp.dot(left, left[:b].T, precision=HIGHEST)
        ljj = jnp.linalg.cholesky(below[:b])
        ijj = jax.scipy.linalg.solve_triangular(ljj, jnp.eye(b, dtype=F32), lower=True)
        rest = jnp.dot(below[b:], ijj.T, precision=HIGHEST)
        cols.append(jnp.concatenate([jnp.tril(ljj), rest], axis=0))
        invs.append(ijj)
        if j == sync_after:
            (cols, invs), _ = lax.optimization_barrier(((cols, invs), anchor))
    lower = jnp.concatenate(
        [jnp.pad(cl, ((k * b, 0), (0, 0))) for k, cl in enumerate(cols)], axis=1)
    linv = invs[0]
    for i in range(1, nb):
        lo, hi = i * b, (i + 1) * b
        row = -jnp.dot(invs[i], jnp.dot(lower[lo:hi, :lo], linv, precision=HIGHEST), precision=HIGHEST)
        top = jnp.pad(linv, ((0, 0), (0, b)))
        bottom = jnp.concatenate([row, invs[i]], axis=1)
        linv = jnp.concatenate([top, bottom], axis=0)
    return lower, linv


def shards(panel_rows, diag_blocks, adjoint, fill):
    n_col = lax.axis_size("col")
    n_pan = lax.axis_size("panel")
    c = lax.axis_index("col")
    p = lax.axis_index("panel")
    piece, width = panel_rows.shape

    flat = n_pan * n_col
    perm = [((dst % n_col) * n_pan + dst // n_col, dst) for dst in range(flat)]
    mine = lax.ppermute(panel_rows, ("panel", "col"), perm)
    col_rows = lax.all_gather(mine, "panel", axis=0, tiled=True)

    marks = fill.astype(BF16)
    col_blocks = fill.shape[1]
    per = piece // B

    def product(k):
        rows = lax.dynamic_slice_in_dim(adjoint, k * piece, piece, 0)
        m = lax.dynamic_slice_in_dim(marks, k * per, per, 0)
        masked = (rows.reshape(per, B, col_blocks, B) * m[:, None, :, None]).reshape(piece, -1)
        return jnp.dot(masked, col_rows, preferred_element_type=F32)

    parts = [product((c + s) % n_col) for s in range(n_col)]
    total = parts[0]
    for s in range(1, n_col):
        total = total + shift(parts[s], "col", n_col, s)
    moment = jnp.dot(total.T, panel_rows.astype(F32), precision=HIGHEST)
    stages = [("panel", n_pan, p, 1)]
    stages += [("col", n_col, c, 1 << k) for k in range(n_col.bit_length() - 1)]
    stages += [("panel", n_pan, p, 1 << k) for k in range(1, n_pan.bit_length() - 1)]
    lower, linv = factor_and_inverse(diag_blocks, parts, 2)
    minv = jnp.dot(linv.T, linv, precision=HIGHEST)
    moment, (lower, linv, minv) = lax.optimization_barrier((moment, (lower, linv, minv)))
    moment = halving_sum(moment, stages)

    grad_panel = -jnp.dot(total, minv, precision=HIGHEST)
    grad_lower = jnp.tril(jnp.dot(jnp.dot(minv, moment, precision=HIGHEST), linv.T, precision=HIGHEST))

    diag = jnp.diagonal(lower)
    eye = jnp.eye(width, dtype=F32)
    bar = grad_lower + eye * (2.0 / diag)[None, :]
    inner = jnp.tril(jnp.dot(lower.T, bar, precision=HIGHEST)) * (1.0 - 0.5 * eye)
    sigma = jnp.dot(jnp.dot(linv.T, inner, precision=HIGHEST), linv, precision=HIGHEST)
    grad_diag = 0.5 * (sigma + sigma.T)
    return (grad_panel, grad_diag)


def solution(mesh):
    in_specs = (P(("panel", "col"), None), P(), P("panel", "col"), P("panel", "col"))
    out_specs = (P(("panel", "col"), None), P())
    return jax.shard_map(shards, mesh=mesh, in_specs=in_specs, out_specs=out_specs, check_vma=False)
```

```python
import jax
import jax.numpy as jnp
from jax import lax
from jax.sharding import PartitionSpec as P

B = 256
F32 = jnp.float32
BF16 = jnp.bfloat16
HIGHEST = lax.Precision.HIGHEST


def shift(x, axis, n, s):
    return lax.ppermute(x, axis, [(i, (i + s) % n) for i in range(n)])


def gather_ring(x, axis, n, me):
    got = [x] + [shift(x, axis, n, s) for s in range(1, n)]
    held = jnp.stack([got[(-m) % n] for m in range(n)])
    return jnp.roll(held, me, axis=0).reshape((-1,) + x.shape[1:])


def scatter_sum(x, axis, n, me):
    rows = x.shape[0] // n
    acc = lax.dynamic_slice_in_dim(x, me * rows, rows, 0)
    for s in range(1, n):
        part = lax.dynamic_slice_in_dim(x, ((me + s) % n) * rows, rows, 0)
        acc = acc + shift(part, axis, n, s)
    return acc


def all_sum(x, n_col, n_pan, c, p):
    y = scatter_sum(x, "col", n_col, c)
    z = scatter_sum(y, "panel", n_pan, p)
    y = gather_ring(z, "panel", n_pan, p)
    return gather_ring(y, "col", n_col, c)


def split3(w):
    hi = lax.reduce_precision(w, exponent_bits=8, mantissa_bits=7)
    r = w - hi
    mid = lax.reduce_precision(r, exponent_bits=8, mantissa_bits=7)
    lo = r - mid
    return hi.astype(BF16), mid.astype(BF16), lo.astype(BF16)


def apply_split(x, parts):
    hi, mid, lo = parts
    d = lambda w: jnp.dot(x, w, preferred_element_type=F32)
    return d(hi) + (d(mid) + d(lo))


def halving_sum(x, stages):
    bits = []
    for axis, n, me, b in stages:
        bit = (me // b) % 2
        pairs = [(i, i ^ b) for i in range(n)]
        h = x.shape[0] // 2
        keep = lax.dynamic_slice_in_dim(x, bit * h, h, 0)
        send = lax.dynamic_slice_in_dim(x, (1 - bit) * h, h, 0)
        x = keep + lax.ppermute(send, axis, pairs)
        bits.append((axis, pairs, bit))
    for axis, pairs, bit in reversed(bits):
        other = lax.ppermute(x, axis, pairs)
        x = jnp.where(bit == 0, jnp.concatenate([x, other]), jnp.concatenate([other, x]))
    return x


def factor_and_inverse(matrix, anchor, sync_after, b=128):
    n = matrix.shape[0]
    nb = n // b
    a = 0.5 * (matrix + matrix.T)
    cols = []
    invs = []
    for j in range(nb):
        lo, hi = j * b, (j + 1) * b
        below = a[lo:, lo:hi]
        if j > 0:
            left = jnp.concatenate([cl[lo - k * b:] for k, cl in enumerate(cols)], axis=1)
            below = below - jnp.dot(left, left[:b].T, precision=HIGHEST)
        ljj = jnp.linalg.cholesky(below[:b])
        ijj = jax.scipy.linalg.solve_triangular(ljj, jnp.eye(b, dtype=F32), lower=True)
        rest = jnp.dot(below[b:], ijj.T, precision=HIGHEST)
        cols.append(jnp.concatenate([jnp.tril(ljj), rest], axis=0))
        invs.append(ijj)
        if j == sync_after:
            (cols, invs), _ = lax.optimization_barrier(((cols, invs), anchor))
    lower = jnp.concatenate(
        [jnp.pad(cl, ((k * b, 0), (0, 0))) for k, cl in enumerate(cols)], axis=1)
    linv = invs[0]
    for i in range(1, nb):
        lo, hi = i * b, (i + 1) * b
        row = -jnp.dot(invs[i], jnp.dot(lower[lo:hi, :lo], linv, precision=HIGHEST), precision=HIGHEST)
        top = jnp.pad(linv, ((0, 0), (0, b)))
        bottom = jnp.concatenate([row, invs[i]], axis=1)
        linv = jnp.concatenate([top, bottom], axis=0)
    return lower, linv


def shards(panel_rows, diag_blocks, adjoint, fill):
    n_col = lax.axis_size("col")
    n_pan = lax.axis_size("panel")
    c = lax.axis_index("col")
    p = lax.axis_index("panel")
    piece, width = panel_rows.shape

    flat = n_pan * n_col
    perm = [((dst % n_col) * n_pan + dst // n_col, dst) for dst in range(flat)]
    mine = lax.ppermute(panel_rows, ("panel", "col"), perm)
    col_rows = lax.all_gather(mine, "panel", axis=0, tiled=True)

    marks = fill.astype(BF16)
    col_blocks = fill.shape[1]
    per = piece // B

    def product(k):
        rows = lax.dynamic_slice_in_dim(adjoint, k * piece, piece, 0)
        m = lax.dynamic_slice_in_dim(marks, k * per, per, 0)
        masked = (rows.reshape(per, B, col_blocks, B) * m[:, None, :, None]).reshape(piece, -1)
        return jnp.dot(masked, col_rows, preferred_element_type=F32)

    parts = [product((c + s) % n_col) for s in range(n_col)]
    total = parts[0]
    for s in range(1, n_col):
        total = total + shift(parts[s], "col", n_col, s)
    moment = jnp.dot(total.T, panel_rows.astype(F32), precision=HIGHEST)
    stages = [("panel", n_pan, p, 1)]
    stages += [("col", n_col, c, 1 << k) for k in range(n_col.bit_length() - 1)]
    stages += [("panel", n_pan, p, 1 << k) for k in range(1, n_pan.bit_length() - 1)]
    moment = halving_sum(moment, stages)

    lower, linv = factor_and_inverse(diag_blocks, parts, 1)
    minv = jnp.dot(linv.T, linv, precision=HIGHEST)
    grad_panel = -jnp.dot(total, minv, precision=HIGHEST)
    grad_lower = jnp.tril(jnp.dot(jnp.dot(minv, moment, precision=HIGHEST), linv.T, precision=HIGHEST))

    eye = jnp.eye(width, dtype=F32)
    diag = jnp.sum(lower * eye, axis=0)
    half = 1.0 - 0.5 * eye

    def pullback(bar):
        inner = jnp.tril(jnp.dot(lower.T, bar, precision=HIGHEST)) * half
        sigma = jnp.dot(jnp.dot(linv.T, inner, precision=HIGHEST), linv, precision=HIGHEST)
        return 0.5 * (sigma + sigma.T)

    grad_diag = pullback(grad_lower) + pullback(eye * (2.0 / diag)[None, :])
    return (grad_panel, grad_diag)


def solution(mesh):
    in_specs = (P(("panel", "col"), None), P(), P("panel", "col"), P("panel", "col"))
    out_specs = (P(("panel", "col"), None), P())
    return jax.shard_map(shards, mesh=mesh, in_specs=in_specs, out_specs=out_specs, check_vma=False)
```

```python
import jax
import jax.numpy as jnp
from jax import lax
from jax.sharding import PartitionSpec as P

B = 256
F32 = jnp.float32
BF16 = jnp.bfloat16
HIGHEST = lax.Precision.HIGHEST
HIGH = lax.Precision.HIGH


def shift(x, axis, n, s):
    return lax.ppermute(x, axis, [(i, (i + s) % n) for i in range(n)])


def gather_ring(x, axis, n, me):
    got = [x] + [shift(x, axis, n, s) for s in range(1, n)]
    held = jnp.stack([got[(-m) % n] for m in range(n)])
    return jnp.roll(held, me, axis=0).reshape((-1,) + x.shape[1:])


def scatter_sum(x, axis, n, me):
    rows = x.shape[0] // n
    acc = lax.dynamic_slice_in_dim(x, me * rows, rows, 0)
    for s in range(1, n):
        part = lax.dynamic_slice_in_dim(x, ((me + s) % n) * rows, rows, 0)
        acc = acc + shift(part, axis, n, s)
    return acc


def all_sum(x, n_col, n_pan, c, p):
    y = scatter_sum(x, "col", n_col, c)
    z = scatter_sum(y, "panel", n_pan, p)
    y = gather_ring(z, "panel", n_pan, p)
    return gather_ring(y, "col", n_col, c)


def split3(w):
    hi = lax.reduce_precision(w, exponent_bits=8, mantissa_bits=7)
    r = w - hi
    mid = lax.reduce_precision(r, exponent_bits=8, mantissa_bits=7)
    lo = r - mid
    return hi.astype(BF16), mid.astype(BF16), lo.astype(BF16)


def apply_split(x, parts):
    hi, mid, lo = parts
    d = lambda w: jnp.dot(x, w, preferred_element_type=F32)
    return d(hi) + (d(mid) + d(lo))


def halving_sum(x, stages):
    bits = []
    for axis, n, me, b in stages:
        bit = (me // b) % 2
        pairs = [(i, i ^ b) for i in range(n)]
        h = x.shape[0] // 2
        keep = lax.dynamic_slice_in_dim(x, bit * h, h, 0)
        send = lax.dynamic_slice_in_dim(x, (1 - bit) * h, h, 0)
        x = keep + lax.ppermute(send, axis, pairs)
        bits.append((axis, pairs, bit))
    for axis, pairs, bit in reversed(bits):
        other = lax.ppermute(x, axis, pairs)
        x = jnp.where(bit == 0, jnp.concatenate([x, other]), jnp.concatenate([other, x]))
    return x


def factor_and_inverse(matrix, anchor, sync_after, b=128):
    n = matrix.shape[0]
    nb = n // b
    a = 0.5 * (matrix + matrix.T)
    cols = []
    invs = []
    for j in range(nb):
        lo, hi = j * b, (j + 1) * b
        below = a[lo:, lo:hi]
        if j > 0:
            left = jnp.concatenate([cl[lo - k * b:] for k, cl in enumerate(cols)], axis=1)
            below = below - jnp.dot(left, left[:b].T, precision=HIGHEST)
        ljj = jnp.linalg.cholesky(below[:b])
        ijj = jax.scipy.linalg.solve_triangular(ljj, jnp.eye(b, dtype=F32), lower=True)
        rest = jnp.dot(below[b:], ijj.T, precision=HIGHEST)
        cols.append(jnp.concatenate([jnp.tril(ljj), rest], axis=0))
        invs.append(ijj)
        if j == sync_after:
            (cols, invs), _ = lax.optimization_barrier(((cols, invs), anchor))
    lower = jnp.concatenate(
        [jnp.pad(cl, ((k * b, 0), (0, 0))) for k, cl in enumerate(cols)], axis=1)
    linv = invs[0]
    for i in range(1, nb):
        lo, hi = i * b, (i + 1) * b
        row = -jnp.dot(invs[i], jnp.dot(lower[lo:hi, :lo], linv, precision=HIGHEST), precision=HIGHEST)
        top = jnp.pad(linv, ((0, 0), (0, b)))
        bottom = jnp.concatenate([row, invs[i]], axis=1)
        linv = jnp.concatenate([top, bottom], axis=0)
    return lower, linv


def shards(panel_rows, diag_blocks, adjoint, fill):
    n_col = lax.axis_size("col")
    n_pan = lax.axis_size("panel")
    c = lax.axis_index("col")
    p = lax.axis_index("panel")
    piece, width = panel_rows.shape

    flat = n_pan * n_col
    perm = [((dst % n_col) * n_pan + dst // n_col, dst) for dst in range(flat)]
    mine = lax.ppermute(panel_rows, ("panel", "col"), perm)
    col_rows = lax.all_gather(mine, "panel", axis=0, tiled=True)

    marks = fill.astype(BF16)
    col_blocks = fill.shape[1]
    per = piece // B

    def product(k):
        rows = lax.dynamic_slice_in_dim(adjoint, k * piece, piece, 0)
        m = lax.dynamic_slice_in_dim(marks, k * per, per, 0)
        masked = (rows.reshape(per, B, col_blocks, B) * m[:, None, :, None]).reshape(piece, -1)
        return jnp.dot(masked, col_rows, preferred_element_type=F32)

    parts = [product((c + s) % n_col) for s in range(n_col)]
    total = parts[0]
    for s in range(1, n_col):
        total = total + shift(parts[s], "col", n_col, s)
    moment = jnp.dot(total.T, panel_rows.astype(F32), precision=HIGHEST)
    stages = [("panel", n_pan, p, 1)]
    stages += [("col", n_col, c, 1 << k) for k in range(n_col.bit_length() - 1)]
    stages += [("panel", n_pan, p, 1 << k) for k in range(1, n_pan.bit_length() - 1)]
    moment = halving_sum(moment, stages)

    lower, linv = factor_and_inverse(diag_blocks, parts, 1)
    minv = jnp.dot(linv.T, linv, precision=HIGH)
    grad_panel = -jnp.dot(total, minv, precision=HIGH)
    grad_lower = jnp.tril(jnp.dot(jnp.dot(minv, moment, precision=HIGH), linv.T, precision=HIGH))

    eye = jnp.eye(width, dtype=F32)
    diag = jnp.sum(lower * eye, axis=0)
    half = 1.0 - 0.5 * eye

    def pullback(bar):
        inner = jnp.tril(jnp.dot(lower.T, bar, precision=HIGH)) * half
        sigma = jnp.dot(jnp.dot(linv.T, inner, precision=HIGH), linv, precision=HIGH)
        return 0.5 * (sigma + sigma.T)

    grad_diag = pullback(grad_lower) + pullback(eye * (2.0 / diag)[None, :])
    return (grad_panel, grad_diag)


def solution(mesh):
    in_specs = (P(("panel", "col"), None), P(), P("panel", "col"), P("panel", "col"))
    out_specs = (P(("panel", "col"), None), P())
    return jax.shard_map(shards, mesh=mesh, in_specs=in_specs, out_specs=out_specs, check_vma=False)
```

```python
import jax
import jax.numpy as jnp
from jax import lax
from jax.sharding import PartitionSpec as P

B = 256
F32 = jnp.float32
BF16 = jnp.bfloat16
HIGHEST = lax.Precision.HIGHEST
HIGH = lax.Precision.HIGH


def shift(x, axis, n, s):
    return lax.ppermute(x, axis, [(i, (i + s) % n) for i in range(n)])


def gather_ring(x, axis, n, me):
    got = [x] + [shift(x, axis, n, s) for s in range(1, n)]
    held = jnp.stack([got[(-m) % n] for m in range(n)])
    return jnp.roll(held, me, axis=0).reshape((-1,) + x.shape[1:])


def scatter_sum(x, axis, n, me):
    rows = x.shape[0] // n
    acc = lax.dynamic_slice_in_dim(x, me * rows, rows, 0)
    for s in range(1, n):
        part = lax.dynamic_slice_in_dim(x, ((me + s) % n) * rows, rows, 0)
        acc = acc + shift(part, axis, n, s)
    return acc


def all_sum(x, n_col, n_pan, c, p):
    y = scatter_sum(x, "col", n_col, c)
    z = scatter_sum(y, "panel", n_pan, p)
    y = gather_ring(z, "panel", n_pan, p)
    return gather_ring(y, "col", n_col, c)


def split3(w):
    hi = lax.reduce_precision(w, exponent_bits=8, mantissa_bits=7)
    r = w - hi
    mid = lax.reduce_precision(r, exponent_bits=8, mantissa_bits=7)
    lo = r - mid
    return hi.astype(BF16), mid.astype(BF16), lo.astype(BF16)


def apply_split(x, parts):
    hi, mid, lo = parts
    d = lambda w: jnp.dot(x, w, preferred_element_type=F32)
    return d(hi) + (d(mid) + d(lo))


def halving_sum(x, stages, exchange):
    bits = []
    for axis, n, me, b in stages:
        bit = (me // b) % 2
        pairs = [(i, i ^ b) for i in range(n)]
        h = x.shape[0] // 2
        keep = lax.dynamic_slice_in_dim(x, bit * h, h, 0)
        send = lax.dynamic_slice_in_dim(x, (1 - bit) * h, h, 0)
        x = keep + lax.ppermute(send, axis, pairs)
        bits.append((axis, pairs, bit))
    for axis, n, me, b in exchange:
        x = x + lax.ppermute(x, axis, [(i, i ^ b) for i in range(n)])
    for axis, pairs, bit in reversed(bits):
        other = lax.ppermute(x, axis, pairs)
        x = jnp.where(bit == 0, jnp.concatenate([x, other]), jnp.concatenate([other, x]))
    return x


def factor_and_inverse(matrix, anchor, sync_after, b=128):
    n = matrix.shape[0]
    nb = n // b
    a = 0.5 * (matrix + matrix.T)
    cols = []
    invs = []
    for j in range(nb):
        lo, hi = j * b, (j + 1) * b
        below = a[lo:, lo:hi]
        if j > 0:
            left = jnp.concatenate([cl[lo - k * b:] for k, cl in enumerate(cols)], axis=1)
            below = below - jnp.dot(left, left[:b].T, precision=HIGHEST)
        ljj = jnp.linalg.cholesky(below[:b])
        ijj = jax.scipy.linalg.solve_triangular(ljj, jnp.eye(b, dtype=F32), lower=True)
        rest = jnp.dot(below[b:], ijj.T, precision=HIGHEST)
        cols.append(jnp.concatenate([jnp.tril(ljj), rest], axis=0))
        invs.append(ijj)
        if j == sync_after:
            (cols, invs), _ = lax.optimization_barrier(((cols, invs), anchor))
    lower = jnp.concatenate(
        [jnp.pad(cl, ((k * b, 0), (0, 0))) for k, cl in enumerate(cols)], axis=1)
    linv = invs[0]
    for i in range(1, nb):
        lo, hi = i * b, (i + 1) * b
        row = -jnp.dot(invs[i], jnp.dot(lower[lo:hi, :lo], linv, precision=HIGHEST), precision=HIGHEST)
        top = jnp.pad(linv, ((0, 0), (0, b)))
        bottom = jnp.concatenate([row, invs[i]], axis=1)
        linv = jnp.concatenate([top, bottom], axis=0)
    return lower, linv


def shards(panel_rows, diag_blocks, adjoint, fill):
    n_col = lax.axis_size("col")
    n_pan = lax.axis_size("panel")
    c = lax.axis_index("col")
    p = lax.axis_index("panel")
    piece, width = panel_rows.shape

    flat = n_pan * n_col
    perm = [((dst % n_col) * n_pan + dst // n_col, dst) for dst in range(flat)]
    mine = lax.ppermute(panel_rows, ("panel", "col"), perm)
    col_rows = lax.all_gather(mine, "panel", axis=0, tiled=True)

    marks = fill.astype(BF16)
    col_blocks = fill.shape[1]
    per = piece // B

    def product(k):
        rows = lax.dynamic_slice_in_dim(adjoint, k * piece, piece, 0)
        m = lax.dynamic_slice_in_dim(marks, k * per, per, 0)
        masked = (rows.reshape(per, B, col_blocks, B) * m[:, None, :, None]).reshape(piece, -1)
        return jnp.dot(masked, col_rows, preferred_element_type=F32)

    parts = [product((c + s) % n_col) for s in range(n_col)]
    total = parts[0]
    for s in range(1, n_col):
        total = total + shift(parts[s], "col", n_col, s)
    moment = jnp.dot(total.T, panel_rows.astype(F32), precision=HIGHEST)
    stages = [("col", n_col, c, 1 << k) for k in range(n_col.bit_length() - 1)]
    exchange = [("panel", n_pan, p, 1 << k) for k in range(n_pan.bit_length() - 1)]
    moment = halving_sum(moment, stages, exchange)

    lower, linv = factor_and_inverse(diag_blocks, parts, 1)
    minv = jnp.dot(linv.T, linv, precision=HIGH)
    grad_panel = -jnp.dot(total, minv, precision=HIGH)
    grad_lower = jnp.tril(jnp.dot(jnp.dot(minv, moment, precision=HIGH), linv.T, precision=HIGH))

    eye = jnp.eye(width, dtype=F32)
    diag = jnp.sum(lower * eye, axis=0)
    half = 1.0 - 0.5 * eye

    def pullback(bar):
        inner = jnp.tril(jnp.dot(lower.T, bar, precision=HIGH)) * half
        sigma = jnp.dot(jnp.dot(linv.T, inner, precision=HIGH), linv, precision=HIGH)
        return 0.5 * (sigma + sigma.T)

    grad_diag = pullback(grad_lower) + pullback(eye * (2.0 / diag)[None, :])
    return (grad_panel, grad_diag)


def solution(mesh):
    in_specs = (P(("panel", "col"), None), P(), P("panel", "col"), P("panel", "col"))
    out_specs = (P(("panel", "col"), None), P())
    return jax.shard_map(shards, mesh=mesh, in_specs=in_specs, out_specs=out_specs, check_vma=False)
```

```python
import jax
import jax.numpy as jnp
from jax import lax
from jax.sharding import PartitionSpec as P

B = 256
F32 = jnp.float32
BF16 = jnp.bfloat16
HIGHEST = lax.Precision.HIGHEST
HIGH = lax.Precision.HIGH


def shift(x, axis, n, s):
    return lax.ppermute(x, axis, [(i, (i + s) % n) for i in range(n)])


def gather_ring(x, axis, n, me):
    got = [x] + [shift(x, axis, n, s) for s in range(1, n)]
    held = jnp.stack([got[(-m) % n] for m in range(n)])
    return jnp.roll(held, me, axis=0).reshape((-1,) + x.shape[1:])


def scatter_sum(x, axis, n, me):
    rows = x.shape[0] // n
    acc = lax.dynamic_slice_in_dim(x, me * rows, rows, 0)
    for s in range(1, n):
        part = lax.dynamic_slice_in_dim(x, ((me + s) % n) * rows, rows, 0)
        acc = acc + shift(part, axis, n, s)
    return acc


def all_sum(x, n_col, n_pan, c, p):
    y = scatter_sum(x, "col", n_col, c)
    z = scatter_sum(y, "panel", n_pan, p)
    y = gather_ring(z, "panel", n_pan, p)
    return gather_ring(y, "col", n_col, c)


def split3(w):
    hi = lax.reduce_precision(w, exponent_bits=8, mantissa_bits=7)
    r = w - hi
    mid = lax.reduce_precision(r, exponent_bits=8, mantissa_bits=7)
    lo = r - mid
    return hi.astype(BF16), mid.astype(BF16), lo.astype(BF16)


def apply_split(x, parts):
    hi, mid, lo = parts
    d = lambda w: jnp.dot(x, w, preferred_element_type=F32)
    return d(hi) + (d(mid) + d(lo))


def halving_sum(x, stages):
    bits = []
    for axis, n, me, b in stages:
        bit = (me // b) % 2
        pairs = [(i, i ^ b) for i in range(n)]
        h = x.shape[0] // 2
        keep = lax.dynamic_slice_in_dim(x, bit * h, h, 0)
        send = lax.dynamic_slice_in_dim(x, (1 - bit) * h, h, 0)
        x = keep + lax.ppermute(send, axis, pairs)
        bits.append((axis, pairs, bit))
    for axis, pairs, bit in reversed(bits):
        other = lax.ppermute(x, axis, pairs)
        x = jnp.where(bit == 0, jnp.concatenate([x, other]), jnp.concatenate([other, x]))
    return x


def factor_and_inverse(matrix, anchor, sync_after, b=128):
    n = matrix.shape[0]
    nb = n // b
    a = 0.5 * (matrix + matrix.T)
    cols = []
    invs = []
    for j in range(nb):
        lo, hi = j * b, (j + 1) * b
        below = a[lo:, lo:hi]
        if j > 0:
            left = jnp.concatenate([cl[lo - k * b:] for k, cl in enumerate(cols)], axis=1)
            below = below - jnp.dot(left, left[:b].T, precision=HIGHEST)
        ljj = jnp.linalg.cholesky(below[:b])
        ijj = jax.scipy.linalg.solve_triangular(ljj, jnp.eye(b, dtype=F32), lower=True)
        rest = jnp.dot(below[b:], ijj.T, precision=HIGHEST)
        cols.append(jnp.concatenate([jnp.tril(ljj), rest], axis=0))
        invs.append(ijj)
        if j == sync_after:
            (cols, invs), _ = lax.optimization_barrier(((cols, invs), anchor))
    lower = jnp.concatenate(
        [jnp.pad(cl, ((k * b, 0), (0, 0))) for k, cl in enumerate(cols)], axis=1)
    linv = invs[0]
    for i in range(1, nb):
        lo, hi = i * b, (i + 1) * b
        row = -jnp.dot(invs[i], jnp.dot(lower[lo:hi, :lo], linv, precision=HIGHEST), precision=HIGHEST)
        top = jnp.pad(linv, ((0, 0), (0, b)))
        bottom = jnp.concatenate([row, invs[i]], axis=1)
        linv = jnp.concatenate([top, bottom], axis=0)
    return lower, linv


def shards(panel_rows, diag_blocks, adjoint, fill):
    n_col = lax.axis_size("col")
    n_pan = lax.axis_size("panel")
    c = lax.axis_index("col")
    p = lax.axis_index("panel")
    piece, width = panel_rows.shape

    flat = n_pan * n_col
    perm = [((dst % n_col) * n_pan + dst // n_col, dst) for dst in range(flat)]
    mine = lax.ppermute(panel_rows, ("panel", "col"), perm)
    col_rows = lax.all_gather(mine, "panel", axis=0, tiled=True)

    marks = fill.astype(BF16)
    col_blocks = fill.shape[1]
    per = piece // B

    def product(k):
        rows = lax.dynamic_slice_in_dim(adjoint, k * piece, piece, 0)
        m = lax.dynamic_slice_in_dim(marks, k * per, per, 0)
        masked = (rows.reshape(per, B, col_blocks, B) * m[:, None, :, None]).reshape(piece, -1)
        return jnp.dot(masked, col_rows, preferred_element_type=F32)

    parts = [product((c + s) % n_col) for s in range(n_col)]
    total = parts[0]
    for s in range(1, n_col):
        total = total + shift(parts[s], "col", n_col, s)
    moment = jnp.dot(total.T, panel_rows.astype(F32), precision=HIGHEST)
    stages = [("panel", n_pan, p, 1)]
    stages += [("col", n_col, c, 1 << k) for k in range(n_col.bit_length() - 1)]
    stages += [("panel", n_pan, p, 1 << k) for k in range(1, n_pan.bit_length() - 1)]
    lower, linv = factor_and_inverse(diag_blocks, parts, 1)
    minv = jnp.dot(linv.T, linv, precision=HIGH)
    eye = jnp.eye(width, dtype=F32)
    diag = jnp.sum(lower * eye, axis=0)
    half = 1.0 - 0.5 * eye

    def pullback(bar):
        inner = jnp.tril(jnp.dot(lower.T, bar, precision=HIGH)) * half
        sigma = jnp.dot(jnp.dot(linv.T, inner, precision=HIGH), linv, precision=HIGH)
        return 0.5 * (sigma + sigma.T)

    logdet_part = pullback(eye * (2.0 / diag)[None, :])
    moment, (lower, linv, minv, logdet_part) = lax.optimization_barrier(
        (moment, (lower, linv, minv, logdet_part)))
    moment = halving_sum(moment, stages)

    grad_panel = -jnp.dot(total, minv, precision=HIGH)
    grad_lower = jnp.tril(jnp.dot(jnp.dot(minv, moment, precision=HIGH), linv.T, precision=HIGH))

    grad_diag = pullback(grad_lower) + logdet_part
    return (grad_panel, grad_diag)


def solution(mesh):
    in_specs = (P(("panel", "col"), None), P(), P("panel", "col"), P("panel", "col"))
    out_specs = (P(("panel", "col"), None), P())
    return jax.shard_map(shards, mesh=mesh, in_specs=in_specs, out_specs=out_specs, check_vma=False)
```

```python
import jax
import jax.numpy as jnp
from jax import lax
from jax.sharding import PartitionSpec as P

B = 256
F32 = jnp.float32
BF16 = jnp.bfloat16
HIGHEST = lax.Precision.HIGHEST
HIGH = lax.Precision.HIGH


def shift(x, axis, n, s):
    return lax.ppermute(x, axis, [(i, (i + s) % n) for i in range(n)])


def gather_ring(x, axis, n, me):
    got = [x] + [shift(x, axis, n, s) for s in range(1, n)]
    held = jnp.stack([got[(-m) % n] for m in range(n)])
    return jnp.roll(held, me, axis=0).reshape((-1,) + x.shape[1:])


def scatter_sum(x, axis, n, me):
    rows = x.shape[0] // n
    acc = lax.dynamic_slice_in_dim(x, me * rows, rows, 0)
    for s in range(1, n):
        part = lax.dynamic_slice_in_dim(x, ((me + s) % n) * rows, rows, 0)
        acc = acc + shift(part, axis, n, s)
    return acc


def all_sum(x, n_col, n_pan, c, p):
    y = scatter_sum(x, "col", n_col, c)
    z = scatter_sum(y, "panel", n_pan, p)
    y = gather_ring(z, "panel", n_pan, p)
    return gather_ring(y, "col", n_col, c)


def split3(w):
    hi = lax.reduce_precision(w, exponent_bits=8, mantissa_bits=7)
    r = w - hi
    mid = lax.reduce_precision(r, exponent_bits=8, mantissa_bits=7)
    lo = r - mid
    return hi.astype(BF16), mid.astype(BF16), lo.astype(BF16)


def apply_split(x, parts):
    hi, mid, lo = parts
    d = lambda w: jnp.dot(x, w, preferred_element_type=F32)
    return d(hi) + (d(mid) + d(lo))


def halving_sum(x, stages):
    bits = []
    for axis, n, me, b in stages:
        bit = (me // b) % 2
        pairs = [(i, i ^ b) for i in range(n)]
        h = x.shape[0] // 2
        keep = lax.dynamic_slice_in_dim(x, bit * h, h, 0)
        send = lax.dynamic_slice_in_dim(x, (1 - bit) * h, h, 0)
        x = keep + lax.ppermute(send, axis, pairs)
        bits.append((axis, pairs, bit))
    for axis, pairs, bit in reversed(bits):
        other = lax.ppermute(x, axis, pairs)
        x = jnp.where(bit == 0, jnp.concatenate([x, other]), jnp.concatenate([other, x]))
    return x


def factor_and_inverse(matrix, anchor, sync_after, b=128):
    n = matrix.shape[0]
    nb = n // b
    a = 0.5 * (matrix + matrix.T)
    cols = []
    invs = []
    for j in range(nb):
        lo, hi = j * b, (j + 1) * b
        below = a[lo:, lo:hi]
        if j > 0:
            left = jnp.concatenate([cl[lo - k * b:] for k, cl in enumerate(cols)], axis=1)
            below = below - jnp.dot(left, left[:b].T, precision=HIGHEST)
        ljj = jnp.linalg.cholesky(below[:b])
        ijj = jax.scipy.linalg.solve_triangular(ljj, jnp.eye(b, dtype=F32), lower=True)
        rest = jnp.dot(below[b:], ijj.T, precision=HIGHEST)
        cols.append(jnp.concatenate([jnp.tril(ljj), rest], axis=0))
        invs.append(ijj)
        if j == sync_after:
            (cols, invs), _ = lax.optimization_barrier(((cols, invs), anchor))
    lower = jnp.concatenate(
        [jnp.pad(cl, ((k * b, 0), (0, 0))) for k, cl in enumerate(cols)], axis=1)
    linv = invs[0]
    for i in range(1, nb):
        lo, hi = i * b, (i + 1) * b
        row = -jnp.dot(invs[i], jnp.dot(lower[lo:hi, :lo], linv, precision=HIGHEST), precision=HIGHEST)
        top = jnp.pad(linv, ((0, 0), (0, b)))
        bottom = jnp.concatenate([row, invs[i]], axis=1)
        linv = jnp.concatenate([top, bottom], axis=0)
    return lower, linv


def shards(panel_rows, diag_blocks, adjoint, fill):
    n_col = lax.axis_size("col")
    n_pan = lax.axis_size("panel")
    c = lax.axis_index("col")
    p = lax.axis_index("panel")
    piece, width = panel_rows.shape

    flat = n_pan * n_col
    perm = [((dst % n_col) * n_pan + dst // n_col, dst) for dst in range(flat)]
    mine = lax.ppermute(panel_rows, ("panel", "col"), perm)
    col_rows = lax.all_gather(mine, "panel", axis=0, tiled=True)

    marks = fill.astype(BF16)
    col_blocks = fill.shape[1]
    per = piece // B

    def product(k):
        rows = lax.dynamic_slice_in_dim(adjoint, k * piece, piece, 0)
        m = lax.dynamic_slice_in_dim(marks, k * per, per, 0)
        masked = (rows.reshape(per, B, col_blocks, B) * m[:, None, :, None]).reshape(piece, -1)
        return jnp.dot(masked, col_rows, preferred_element_type=F32)

    nx = 4 if n_col % 4 == 0 else n_col
    nz = n_col // nx
    x, z = c % nx, c // nx
    sends = []
    for o in range(1, nx):
        xo = (x + o) % nx
        pair = jnp.concatenate([product(zz * nx + xo) for zz in range(nz)])
        sends.append((o, pair))
    parts = [pair for _, pair in sends]
    acc = jnp.concatenate([product(zz * nx + x) for zz in range(nz)])
    for o, pair in sends:
        acc = acc + lax.ppermute(
            pair, "col", [(i, (i // nx) * nx + (i % nx + o) % nx) for i in range(n_col)])
    total = lax.dynamic_slice_in_dim(acc, z * piece, piece, 0)
    for o in range(1, nz):
        part = lax.dynamic_slice_in_dim(acc, ((z + o) % nz) * piece, piece, 0)
        total = total + lax.ppermute(
            part, "col", [(i, (((i // nx) + o) % nz) * nx + i % nx) for i in range(n_col)])
    moment = jnp.dot(total.T, panel_rows.astype(F32), precision=HIGHEST)
    stages = [("panel", n_pan, p, 1)]
    stages += [("col", n_col, c, 1 << k) for k in range(n_col.bit_length() - 1)]
    stages += [("panel", n_pan, p, 1 << k) for k in range(1, n_pan.bit_length() - 1)]
    moment = halving_sum(moment, stages)

    lower, linv = factor_and_inverse(diag_blocks, parts, 1)
    minv = jnp.dot(linv.T, linv, precision=HIGH)
    grad_panel = -jnp.dot(total, minv, precision=HIGH)
    grad_lower = jnp.tril(jnp.dot(jnp.dot(minv, moment, precision=HIGH), linv.T, precision=HIGH))

    eye = jnp.eye(width, dtype=F32)
    diag = jnp.sum(lower * eye, axis=0)
    half = 1.0 - 0.5 * eye

    def pullback(bar):
        inner = jnp.tril(jnp.dot(lower.T, bar, precision=HIGH)) * half
        sigma = jnp.dot(jnp.dot(linv.T, inner, precision=HIGH), linv, precision=HIGH)
        return 0.5 * (sigma + sigma.T)

    grad_diag = pullback(grad_lower) + pullback(eye * (2.0 / diag)[None, :])
    return (grad_panel, grad_diag)


def solution(mesh):
    in_specs = (P(("panel", "col"), None), P(), P("panel", "col"), P("panel", "col"))
    out_specs = (P(("panel", "col"), None), P())
    return jax.shard_map(shards, mesh=mesh, in_specs=in_specs, out_specs=out_specs, check_vma=False)
```

```python
import jax
import jax.numpy as jnp
from jax import lax
from jax.sharding import PartitionSpec as P

B = 256
F32 = jnp.float32
BF16 = jnp.bfloat16
HIGHEST = lax.Precision.HIGHEST
HIGH = lax.Precision.HIGH


def shift(x, axis, n, s):
    return lax.ppermute(x, axis, [(i, (i + s) % n) for i in range(n)])


def gather_ring(x, axis, n, me):
    got = [x] + [shift(x, axis, n, s) for s in range(1, n)]
    held = jnp.stack([got[(-m) % n] for m in range(n)])
    return jnp.roll(held, me, axis=0).reshape((-1,) + x.shape[1:])


def scatter_sum(x, axis, n, me):
    rows = x.shape[0] // n
    acc = lax.dynamic_slice_in_dim(x, me * rows, rows, 0)
    for s in range(1, n):
        part = lax.dynamic_slice_in_dim(x, ((me + s) % n) * rows, rows, 0)
        acc = acc + shift(part, axis, n, s)
    return acc


def all_sum(x, n_col, n_pan, c, p):
    y = scatter_sum(x, "col", n_col, c)
    z = scatter_sum(y, "panel", n_pan, p)
    y = gather_ring(z, "panel", n_pan, p)
    return gather_ring(y, "col", n_col, c)


def split3(w):
    hi = lax.reduce_precision(w, exponent_bits=8, mantissa_bits=7)
    r = w - hi
    mid = lax.reduce_precision(r, exponent_bits=8, mantissa_bits=7)
    lo = r - mid
    return hi.astype(BF16), mid.astype(BF16), lo.astype(BF16)


def apply_split(x, parts):
    hi, mid, lo = parts
    d = lambda w: jnp.dot(x, w, preferred_element_type=F32)
    return d(hi) + (d(mid) + d(lo))


def halving_sum(x, stages):
    bits = []
    for axis, n, me, b in stages:
        bit = (me // b) % 2
        pairs = [(i, i ^ b) for i in range(n)]
        h = x.shape[0] // 2
        keep = lax.dynamic_slice_in_dim(x, bit * h, h, 0)
        send = lax.dynamic_slice_in_dim(x, (1 - bit) * h, h, 0)
        x = keep + lax.ppermute(send, axis, pairs)
        bits.append((axis, pairs, bit))
    for axis, pairs, bit in reversed(bits):
        other = lax.ppermute(x, axis, pairs)
        x = jnp.where(bit == 0, jnp.concatenate([x, other]), jnp.concatenate([other, x]))
    return x


def factor_and_inverse(matrix, anchor, sync_after, b=128):
    n = matrix.shape[0]
    nb = n // b
    a = 0.5 * (matrix + matrix.T)
    cols = []
    invs = []
    for j in range(nb):
        lo, hi = j * b, (j + 1) * b
        below = a[lo:, lo:hi]
        if j > 0:
            left = jnp.concatenate([cl[lo - k * b:] for k, cl in enumerate(cols)], axis=1)
            below = below - jnp.dot(left, left[:b].T, precision=HIGHEST)
        ljj = jnp.linalg.cholesky(below[:b])
        ijj = jax.scipy.linalg.solve_triangular(ljj, jnp.eye(b, dtype=F32), lower=True)
        rest = jnp.dot(below[b:], ijj.T, precision=HIGHEST)
        cols.append(jnp.concatenate([jnp.tril(ljj), rest], axis=0))
        invs.append(ijj)
        if j == sync_after:
            (cols, invs), _ = lax.optimization_barrier(((cols, invs), anchor))
    lower = jnp.concatenate(
        [jnp.pad(cl, ((k * b, 0), (0, 0))) for k, cl in enumerate(cols)], axis=1)
    linv = invs[0]
    for i in range(1, nb):
        lo, hi = i * b, (i + 1) * b
        row = -jnp.dot(invs[i], jnp.dot(lower[lo:hi, :lo], linv, precision=HIGHEST), precision=HIGHEST)
        top = jnp.pad(linv, ((0, 0), (0, b)))
        bottom = jnp.concatenate([row, invs[i]], axis=1)
        linv = jnp.concatenate([top, bottom], axis=0)
    return lower, linv


def shards(panel_rows, diag_blocks, adjoint, fill):
    n_col = lax.axis_size("col")
    n_pan = lax.axis_size("panel")
    c = lax.axis_index("col")
    p = lax.axis_index("panel")
    piece, width = panel_rows.shape

    flat = n_pan * n_col
    perm = [((dst % n_col) * n_pan + dst // n_col, dst) for dst in range(flat)]
    mine = lax.ppermute(panel_rows, ("panel", "col"), perm)
    col_rows = lax.all_gather(mine, "panel", axis=0, tiled=True)

    marks = fill.astype(BF16)
    col_blocks = fill.shape[1]
    per = piece // B

    n_rows = adjoint.shape[0]
    masked = (adjoint.reshape(n_rows // B, B, col_blocks, B) * marks[:, None, :, None]).reshape(n_rows, -1)
    masked = lax.optimization_barrier(masked)

    def product(k):
        rows = lax.dynamic_slice_in_dim(masked, k * piece, piece, 0)
        return jnp.dot(rows, col_rows, preferred_element_type=F32)

    parts = [product((c + s) % n_col) for s in range(n_col)]
    total = parts[0]
    for s in range(1, n_col):
        total = total + shift(parts[s], "col", n_col, s)
    moment = jnp.dot(total.T, panel_rows.astype(F32), precision=HIGHEST)
    stages = [("panel", n_pan, p, 1)]
    stages += [("col", n_col, c, 1 << k) for k in range(n_col.bit_length() - 1)]
    stages += [("panel", n_pan, p, 1 << k) for k in range(1, n_pan.bit_length() - 1)]
    moment = halving_sum(moment, stages)

    lower, linv = factor_and_inverse(diag_blocks, parts, 1)
    minv = jnp.dot(linv.T, linv, precision=HIGH)
    grad_panel = -jnp.dot(total, minv, precision=HIGH)
    grad_lower = jnp.tril(jnp.dot(jnp.dot(minv, moment, precision=HIGH), linv.T, precision=HIGH))

    eye = jnp.eye(width, dtype=F32)
    diag = jnp.sum(lower * eye, axis=0)
    half = 1.0 - 0.5 * eye

    def pullback(bar):
        inner = jnp.tril(jnp.dot(lower.T, bar, precision=HIGH)) * half
        sigma = jnp.dot(jnp.dot(linv.T, inner, precision=HIGH), linv, precision=HIGH)
        return 0.5 * (sigma + sigma.T)

    grad_diag = pullback(grad_lower) + pullback(eye * (2.0 / diag)[None, :])
    return (grad_panel, grad_diag)


def solution(mesh):
    in_specs = (P(("panel", "col"), None), P(), P("panel", "col"), P("panel", "col"))
    out_specs = (P(("panel", "col"), None), P())
    return jax.shard_map(shards, mesh=mesh, in_specs=in_specs, out_specs=out_specs, check_vma=False)
```

```python
import jax
import jax.numpy as jnp
from jax import lax
from jax.sharding import PartitionSpec as P

B = 256
F32 = jnp.float32
BF16 = jnp.bfloat16
HIGHEST = lax.Precision.HIGHEST
HIGH = lax.Precision.HIGH


def shift(x, axis, n, s):
    return lax.ppermute(x, axis, [(i, (i + s) % n) for i in range(n)])


def gather_ring(x, axis, n, me):
    got = [x] + [shift(x, axis, n, s) for s in range(1, n)]
    held = jnp.stack([got[(-m) % n] for m in range(n)])
    return jnp.roll(held, me, axis=0).reshape((-1,) + x.shape[1:])


def scatter_sum(x, axis, n, me):
    rows = x.shape[0] // n
    acc = lax.dynamic_slice_in_dim(x, me * rows, rows, 0)
    for s in range(1, n):
        part = lax.dynamic_slice_in_dim(x, ((me + s) % n) * rows, rows, 0)
        acc = acc + shift(part, axis, n, s)
    return acc


def all_sum(x, n_col, n_pan, c, p):
    y = scatter_sum(x, "col", n_col, c)
    z = scatter_sum(y, "panel", n_pan, p)
    y = gather_ring(z, "panel", n_pan, p)
    return gather_ring(y, "col", n_col, c)


def split3(w):
    hi = lax.reduce_precision(w, exponent_bits=8, mantissa_bits=7)
    r = w - hi
    mid = lax.reduce_precision(r, exponent_bits=8, mantissa_bits=7)
    lo = r - mid
    return hi.astype(BF16), mid.astype(BF16), lo.astype(BF16)


def apply_split(x, parts):
    hi, mid, lo = parts
    d = lambda w: jnp.dot(x, w, preferred_element_type=F32)
    return d(hi) + (d(mid) + d(lo))


def halving_sum(x, stages):
    bits = []
    for axis, n, me, b in stages:
        bit = (me // b) % 2
        pairs = [(i, i ^ b) for i in range(n)]
        h = x.shape[0] // 2
        keep = lax.dynamic_slice_in_dim(x, bit * h, h, 0)
        send = lax.dynamic_slice_in_dim(x, (1 - bit) * h, h, 0)
        x = keep + lax.ppermute(send, axis, pairs)
        bits.append((axis, pairs, bit))
    for axis, pairs, bit in reversed(bits):
        other = lax.ppermute(x, axis, pairs)
        x = jnp.where(bit == 0, jnp.concatenate([x, other]), jnp.concatenate([other, x]))
    return x


def factor_and_inverse(matrix, anchor, sync_after, b=128):
    n = matrix.shape[0]
    nb = n // b
    a = 0.5 * (matrix + matrix.T)
    cols = []
    invs = []
    for j in range(nb):
        lo, hi = j * b, (j + 1) * b
        below = a[lo:, lo:hi]
        if j > 0:
            left = jnp.concatenate([cl[lo - k * b:] for k, cl in enumerate(cols)], axis=1)
            below = below - jnp.dot(left, left[:b].T, precision=HIGHEST)
        ljj = jnp.linalg.cholesky(below[:b])
        ijj = jax.scipy.linalg.solve_triangular(ljj, jnp.eye(b, dtype=F32), lower=True)
        rest = jnp.dot(below[b:], ijj.T, precision=HIGHEST)
        cols.append(jnp.concatenate([jnp.tril(ljj), rest], axis=0))
        invs.append(ijj)
        if j == sync_after:
            (cols, invs), _ = lax.optimization_barrier(((cols, invs), anchor))
    lower = jnp.concatenate(
        [jnp.pad(cl, ((k * b, 0), (0, 0))) for k, cl in enumerate(cols)], axis=1)
    linv = invs[0]
    for i in range(1, nb):
        lo, hi = i * b, (i + 1) * b
        row = -jnp.dot(invs[i], jnp.dot(lower[lo:hi, :lo], linv, precision=HIGHEST), precision=HIGHEST)
        top = jnp.pad(linv, ((0, 0), (0, b)))
        bottom = jnp.concatenate([row, invs[i]], axis=1)
        linv = jnp.concatenate([top, bottom], axis=0)
    return lower, linv


def shards(panel_rows, diag_blocks, adjoint, fill):
    n_col = lax.axis_size("col")
    n_pan = lax.axis_size("panel")
    c = lax.axis_index("col")
    p = lax.axis_index("panel")
    piece, width = panel_rows.shape

    flat = n_pan * n_col
    perm = [((dst % n_col) * n_pan + dst // n_col, dst) for dst in range(flat)]
    mine = lax.ppermute(panel_rows, ("panel", "col"), perm)
    col_rows = lax.all_gather(mine, "panel", axis=0, tiled=True)

    marks = fill.astype(BF16)
    col_blocks = fill.shape[1]
    per = piece // B

    n_rows = adjoint.shape[0]
    masked = (adjoint.reshape(n_rows // B, B, col_blocks, B) * marks[:, None, :, None]).reshape(n_rows, -1)
    whole = jnp.dot(masked, col_rows, preferred_element_type=F32)

    def product(k):
        return lax.dynamic_slice_in_dim(whole, k * piece, piece, 0)

    parts = [product((c + s) % n_col) for s in range(n_col)]
    total = parts[0]
    for s in range(1, n_col):
        total = total + shift(parts[s], "col", n_col, s)
    moment = jnp.dot(total.T, panel_rows.astype(F32), precision=HIGHEST)
    stages = [("panel", n_pan, p, 1)]
    stages += [("col", n_col, c, 1 << k) for k in range(n_col.bit_length() - 1)]
    stages += [("panel", n_pan, p, 1 << k) for k in range(1, n_pan.bit_length() - 1)]
    moment = halving_sum(moment, stages)

    lower, linv = factor_and_inverse(diag_blocks, parts, 1)
    minv = jnp.dot(linv.T, linv, precision=HIGH)
    grad_panel = -jnp.dot(total, minv, precision=HIGH)
    grad_lower = jnp.tril(jnp.dot(jnp.dot(minv, moment, precision=HIGH), linv.T, precision=HIGH))

    eye = jnp.eye(width, dtype=F32)
    diag = jnp.sum(lower * eye, axis=0)
    half = 1.0 - 0.5 * eye

    def pullback(bar):
        inner = jnp.tril(jnp.dot(lower.T, bar, precision=HIGH)) * half
        sigma = jnp.dot(jnp.dot(linv.T, inner, precision=HIGH), linv, precision=HIGH)
        return 0.5 * (sigma + sigma.T)

    grad_diag = pullback(grad_lower) + pullback(eye * (2.0 / diag)[None, :])
    return (grad_panel, grad_diag)


def solution(mesh):
    in_specs = (P(("panel", "col"), None), P(), P("panel", "col"), P("panel", "col"))
    out_specs = (P(("panel", "col"), None), P())
    return jax.shard_map(shards, mesh=mesh, in_specs=in_specs, out_specs=out_specs, check_vma=False)
```

```python
import jax
import jax.numpy as jnp
from jax import lax
from jax.sharding import PartitionSpec as P

B = 256
F32 = jnp.float32
BF16 = jnp.bfloat16
HIGHEST = lax.Precision.HIGHEST
HIGH = lax.Precision.HIGH


def shift(x, axis, n, s):
    return lax.ppermute(x, axis, [(i, (i + s) % n) for i in range(n)])


def gather_ring(x, axis, n, me):
    got = [x] + [shift(x, axis, n, s) for s in range(1, n)]
    held = jnp.stack([got[(-m) % n] for m in range(n)])
    return jnp.roll(held, me, axis=0).reshape((-1,) + x.shape[1:])


def scatter_sum(x, axis, n, me):
    rows = x.shape[0] // n
    acc = lax.dynamic_slice_in_dim(x, me * rows, rows, 0)
    for s in range(1, n):
        part = lax.dynamic_slice_in_dim(x, ((me + s) % n) * rows, rows, 0)
        acc = acc + shift(part, axis, n, s)
    return acc


def all_sum(x, n_col, n_pan, c, p):
    y = scatter_sum(x, "col", n_col, c)
    z = scatter_sum(y, "panel", n_pan, p)
    y = gather_ring(z, "panel", n_pan, p)
    return gather_ring(y, "col", n_col, c)


def split3(w):
    hi = lax.reduce_precision(w, exponent_bits=8, mantissa_bits=7)
    r = w - hi
    mid = lax.reduce_precision(r, exponent_bits=8, mantissa_bits=7)
    lo = r - mid
    return hi.astype(BF16), mid.astype(BF16), lo.astype(BF16)


def apply_split(x, parts):
    hi, mid, lo = parts
    d = lambda w: jnp.dot(x, w, preferred_element_type=F32)
    return d(hi) + (d(mid) + d(lo))


def halving_sum(x, stages):
    bits = []
    for axis, n, me, b in stages:
        bit = (me // b) % 2
        pairs = [(i, i ^ b) for i in range(n)]
        h = x.shape[0] // 2
        keep = lax.dynamic_slice_in_dim(x, bit * h, h, 0)
        send = lax.dynamic_slice_in_dim(x, (1 - bit) * h, h, 0)
        x = keep + lax.ppermute(send, axis, pairs)
        bits.append((axis, pairs, bit))
    for axis, pairs, bit in reversed(bits):
        other = lax.ppermute(x, axis, pairs)
        x = jnp.where(bit == 0, jnp.concatenate([x, other]), jnp.concatenate([other, x]))
    return x


def factor_and_inverse(matrix, anchor, sync_after, b=128):
    n = matrix.shape[0]
    nb = n // b
    a = 0.5 * (matrix + matrix.T)
    cols = []
    invs = []
    for j in range(nb):
        lo, hi = j * b, (j + 1) * b
        below = a[lo:, lo:hi]
        if j > 0:
            left = jnp.concatenate([cl[lo - k * b:] for k, cl in enumerate(cols)], axis=1)
            below = below - jnp.dot(left, left[:b].T, precision=HIGHEST)
        ljj = jnp.linalg.cholesky(below[:b])
        ijj = jax.scipy.linalg.solve_triangular(ljj, jnp.eye(b, dtype=F32), lower=True)
        rest = jnp.dot(below[b:], ijj.T, precision=HIGHEST)
        cols.append(jnp.concatenate([jnp.tril(ljj), rest], axis=0))
        invs.append(ijj)
        if j == sync_after:
            (cols, invs), _ = lax.optimization_barrier(((cols, invs), anchor))
    lower = jnp.concatenate(
        [jnp.pad(cl, ((k * b, 0), (0, 0))) for k, cl in enumerate(cols)], axis=1)
    linv = invs[0]
    for i in range(1, nb):
        lo, hi = i * b, (i + 1) * b
        row = -jnp.dot(invs[i], jnp.dot(lower[lo:hi, :lo], linv, precision=HIGHEST), precision=HIGHEST)
        top = jnp.pad(linv, ((0, 0), (0, b)))
        bottom = jnp.concatenate([row, invs[i]], axis=1)
        linv = jnp.concatenate([top, bottom], axis=0)
    return lower, linv


def shards(panel_rows, diag_blocks, adjoint, fill):
    n_col = lax.axis_size("col")
    n_pan = lax.axis_size("panel")
    c = lax.axis_index("col")
    p = lax.axis_index("panel")
    piece, width = panel_rows.shape

    flat = n_pan * n_col
    perm = [((dst % n_col) * n_pan + dst // n_col, dst) for dst in range(flat)]
    mine = lax.ppermute(panel_rows, ("panel", "col"), perm)
    col_rows = lax.all_gather(mine, "panel", axis=0, tiled=True)

    marks = fill.astype(BF16)
    col_blocks = fill.shape[1]
    per = piece // B

    def product(k):
        rows = lax.dynamic_slice_in_dim(adjoint, k * piece, piece, 0)
        m = lax.dynamic_slice_in_dim(marks, k * per, per, 0)
        masked = (rows.reshape(per, B, col_blocks, B) * m[:, None, :, None]).reshape(piece, -1)
        return jnp.dot(masked, col_rows, preferred_element_type=F32)

    parts = [product((c + s) % n_col) for s in range(n_col)]
    got = [shift(parts[s], "col", n_col, s) for s in range(1, n_col)]
    total = parts[0]
    for r in got:
        total = total + r
    moment = jnp.dot(total.T, panel_rows.astype(F32), precision=HIGHEST)
    stages = [("panel", n_pan, p, 1)]
    stages += [("col", n_col, c, 1 << k) for k in range(n_col.bit_length() - 1)]
    stages += [("panel", n_pan, p, 1 << k) for k in range(1, n_pan.bit_length() - 1)]
    moment = halving_sum(moment, stages)

    lower, linv = factor_and_inverse(diag_blocks, (parts, got[:2]), 1)
    minv = jnp.dot(linv.T, linv, precision=HIGH)
    grad_panel = -jnp.dot(total, minv, precision=HIGH)
    grad_lower = jnp.tril(jnp.dot(jnp.dot(minv, moment, precision=HIGH), linv.T, precision=HIGH))

    eye = jnp.eye(width, dtype=F32)
    diag = jnp.sum(lower * eye, axis=0)
    half = 1.0 - 0.5 * eye

    def pullback(bar):
        inner = jnp.tril(jnp.dot(lower.T, bar, precision=HIGH)) * half
        sigma = jnp.dot(jnp.dot(linv.T, inner, precision=HIGH), linv, precision=HIGH)
        return 0.5 * (sigma + sigma.T)

    grad_diag = pullback(grad_lower) + pullback(eye * (2.0 / diag)[None, :])
    return (grad_panel, grad_diag)


def solution(mesh):
    in_specs = (P(("panel", "col"), None), P(), P("panel", "col"), P("panel", "col"))
    out_specs = (P(("panel", "col"), None), P())
    return jax.shard_map(shards, mesh=mesh, in_specs=in_specs, out_specs=out_specs, check_vma=False)
```

```python
import jax
import jax.numpy as jnp
from jax import lax
from jax.sharding import PartitionSpec as P

B = 256
F32 = jnp.float32
BF16 = jnp.bfloat16
HIGHEST = lax.Precision.HIGHEST
HIGH = lax.Precision.HIGH


def shift(x, axis, n, s):
    return lax.ppermute(x, axis, [(i, (i + s) % n) for i in range(n)])


def gather_ring(x, axis, n, me):
    got = [x] + [shift(x, axis, n, s) for s in range(1, n)]
    held = jnp.stack([got[(-m) % n] for m in range(n)])
    return jnp.roll(held, me, axis=0).reshape((-1,) + x.shape[1:])


def scatter_sum(x, axis, n, me):
    rows = x.shape[0] // n
    acc = lax.dynamic_slice_in_dim(x, me * rows, rows, 0)
    for s in range(1, n):
        part = lax.dynamic_slice_in_dim(x, ((me + s) % n) * rows, rows, 0)
        acc = acc + shift(part, axis, n, s)
    return acc


def all_sum(x, n_col, n_pan, c, p):
    y = scatter_sum(x, "col", n_col, c)
    z = scatter_sum(y, "panel", n_pan, p)
    y = gather_ring(z, "panel", n_pan, p)
    return gather_ring(y, "col", n_col, c)


def split3(w):
    hi = lax.reduce_precision(w, exponent_bits=8, mantissa_bits=7)
    r = w - hi
    mid = lax.reduce_precision(r, exponent_bits=8, mantissa_bits=7)
    lo = r - mid
    return hi.astype(BF16), mid.astype(BF16), lo.astype(BF16)


def apply_split(x, parts):
    hi, mid, lo = parts
    d = lambda w: jnp.dot(x, w, preferred_element_type=F32)
    return d(hi) + (d(mid) + d(lo))


def halving_sum(x, stages):
    bits = []
    for axis, n, me, b in stages:
        bit = (me // b) % 2
        pairs = [(i, i ^ b) for i in range(n)]
        h = x.shape[0] // 2
        keep = lax.dynamic_slice_in_dim(x, bit * h, h, 0)
        send = lax.dynamic_slice_in_dim(x, (1 - bit) * h, h, 0)
        x = keep + lax.ppermute(send, axis, pairs)
        bits.append((axis, pairs, bit))
    for axis, pairs, bit in reversed(bits):
        other = lax.ppermute(x, axis, pairs)
        x = jnp.where(bit == 0, jnp.concatenate([x, other]), jnp.concatenate([other, x]))
    return x


def factor_and_inverse(matrix, anchor, sync_after, b=128):
    n = matrix.shape[0]
    nb = n // b
    a = 0.5 * (matrix + matrix.T)
    cols = []
    invs = []
    for j in range(nb):
        lo, hi = j * b, (j + 1) * b
        below = a[lo:, lo:hi]
        if j > 0:
            left = jnp.concatenate([cl[lo - k * b:] for k, cl in enumerate(cols)], axis=1)
            below = below - jnp.dot(left, left[:b].T, precision=HIGH)
        ljj = jnp.linalg.cholesky(below[:b])
        ijj = jax.scipy.linalg.solve_triangular(ljj, jnp.eye(b, dtype=F32), lower=True)
        rest = jnp.dot(below[b:], ijj.T, precision=HIGH)
        cols.append(jnp.concatenate([jnp.tril(ljj), rest], axis=0))
        invs.append(ijj)
        if j == sync_after:
            (cols, invs), _ = lax.optimization_barrier(((cols, invs), anchor))
    lower = jnp.concatenate(
        [jnp.pad(cl, ((k * b, 0), (0, 0))) for k, cl in enumerate(cols)], axis=1)
    linv = invs[0]
    for i in range(1, nb):
        lo, hi = i * b, (i + 1) * b
        row = -jnp.dot(invs[i], jnp.dot(lower[lo:hi, :lo], linv, precision=HIGH), precision=HIGH)
        top = jnp.pad(linv, ((0, 0), (0, b)))
        bottom = jnp.concatenate([row, invs[i]], axis=1)
        linv = jnp.concatenate([top, bottom], axis=0)
    return lower, linv


def shards(panel_rows, diag_blocks, adjoint, fill):
    n_col = lax.axis_size("col")
    n_pan = lax.axis_size("panel")
    c = lax.axis_index("col")
    p = lax.axis_index("panel")
    piece, width = panel_rows.shape

    flat = n_pan * n_col
    perm = [((dst % n_col) * n_pan + dst // n_col, dst) for dst in range(flat)]
    mine = lax.ppermute(panel_rows, ("panel", "col"), perm)
    col_rows = lax.all_gather(mine, "panel", axis=0, tiled=True)

    marks = fill.astype(BF16)
    col_blocks = fill.shape[1]
    per = piece // B

    def product(k):
        rows = lax.dynamic_slice_in_dim(adjoint, k * piece, piece, 0)
        m = lax.dynamic_slice_in_dim(marks, k * per, per, 0)
        masked = (rows.reshape(per, B, col_blocks, B) * m[:, None, :, None]).reshape(piece, -1)
        return jnp.dot(masked, col_rows, preferred_element_type=F32)

    parts = [product((c + s) % n_col) for s in range(n_col)]
    total = parts[0]
    for s in range(1, n_col):
        total = total + shift(parts[s], "col", n_col, s)
    moment = jnp.dot(total.T, panel_rows.astype(F32), precision=HIGH)
    stages = [("panel", n_pan, p, 1)]
    stages += [("col", n_col, c, 1 << k) for k in range(n_col.bit_length() - 1)]
    stages += [("panel", n_pan, p, 1 << k) for k in range(1, n_pan.bit_length() - 1)]
    moment = halving_sum(moment, stages)

    lower, linv = factor_and_inverse(diag_blocks, parts, 1)
    minv = jnp.dot(linv.T, linv, precision=HIGH)
    grad_panel = -jnp.dot(total, minv, precision=HIGH)
    grad_lower = jnp.tril(jnp.dot(jnp.dot(minv, moment, precision=HIGH), linv.T, precision=HIGH))

    eye = jnp.eye(width, dtype=F32)
    diag = jnp.sum(lower * eye, axis=0)
    half = 1.0 - 0.5 * eye

    def pullback(bar):
        inner = jnp.tril(jnp.dot(lower.T, bar, precision=HIGH)) * half
        sigma = jnp.dot(jnp.dot(linv.T, inner, precision=HIGH), linv, precision=HIGH)
        return 0.5 * (sigma + sigma.T)

    grad_diag = pullback(grad_lower) + pullback(eye * (2.0 / diag)[None, :])
    return (grad_panel, grad_diag)


def solution(mesh):
    in_specs = (P(("panel", "col"), None), P(), P("panel", "col"), P("panel", "col"))
    out_specs = (P(("panel", "col"), None), P())
    return jax.shard_map(shards, mesh=mesh, in_specs=in_specs, out_specs=out_specs, check_vma=False)
```

```python
import jax
import jax.numpy as jnp
from jax import lax
from jax.sharding import PartitionSpec as P

B = 256
F32 = jnp.float32
BF16 = jnp.bfloat16
HIGHEST = lax.Precision.HIGHEST
HIGH = lax.Precision.HIGH


def shift(x, axis, n, s):
    return lax.ppermute(x, axis, [(i, (i + s) % n) for i in range(n)])


def gather_ring(x, axis, n, me):
    got = [x] + [shift(x, axis, n, s) for s in range(1, n)]
    held = jnp.stack([got[(-m) % n] for m in range(n)])
    return jnp.roll(held, me, axis=0).reshape((-1,) + x.shape[1:])


def scatter_sum(x, axis, n, me):
    rows = x.shape[0] // n
    acc = lax.dynamic_slice_in_dim(x, me * rows, rows, 0)
    for s in range(1, n):
        part = lax.dynamic_slice_in_dim(x, ((me + s) % n) * rows, rows, 0)
        acc = acc + shift(part, axis, n, s)
    return acc


def all_sum(x, n_col, n_pan, c, p):
    y = scatter_sum(x, "col", n_col, c)
    z = scatter_sum(y, "panel", n_pan, p)
    y = gather_ring(z, "panel", n_pan, p)
    return gather_ring(y, "col", n_col, c)


def split3(w):
    hi = lax.reduce_precision(w, exponent_bits=8, mantissa_bits=7)
    r = w - hi
    mid = lax.reduce_precision(r, exponent_bits=8, mantissa_bits=7)
    lo = r - mid
    return hi.astype(BF16), mid.astype(BF16), lo.astype(BF16)


def apply_split(x, parts):
    hi, mid, lo = parts
    d = lambda w: jnp.dot(x, w, preferred_element_type=F32)
    return d(hi) + (d(mid) + d(lo))


def halving_sum(x, stages):
    bits = []
    for axis, n, me, b in stages:
        bit = (me // b) % 2
        pairs = [(i, i ^ b) for i in range(n)]
        h = x.shape[0] // 2
        keep = lax.dynamic_slice_in_dim(x, bit * h, h, 0)
        send = lax.dynamic_slice_in_dim(x, (1 - bit) * h, h, 0)
        x = keep + lax.ppermute(send, axis, pairs)
        bits.append((axis, pairs, bit))
    for axis, pairs, bit in reversed(bits):
        other = lax.ppermute(x, axis, pairs)
        x = lax.dynamic_update_slice_in_dim(jnp.concatenate([other, other]), x, bit * x.shape[0], 0)
    return x


def factor_and_inverse(matrix, anchor, sync_after, b=128):
    n = matrix.shape[0]
    nb = n // b
    a = 0.5 * (matrix + matrix.T)
    cols = []
    invs = []
    for j in range(nb):
        lo, hi = j * b, (j + 1) * b
        below = a[lo:, lo:hi]
        if j > 0:
            left = jnp.concatenate([cl[lo - k * b:] for k, cl in enumerate(cols)], axis=1)
            below = below - jnp.dot(left, left[:b].T, precision=HIGH)
        ljj = jnp.linalg.cholesky(below[:b])
        ijj = jax.scipy.linalg.solve_triangular(ljj, jnp.eye(b, dtype=F32), lower=True)
        rest = jnp.dot(below[b:], ijj.T, precision=HIGH)
        cols.append(jnp.concatenate([jnp.tril(ljj), rest], axis=0))
        invs.append(ijj)
        if j == sync_after:
            (cols, invs), _ = lax.optimization_barrier(((cols, invs), anchor))
    lower = jnp.concatenate(
        [jnp.pad(cl, ((k * b, 0), (0, 0))) for k, cl in enumerate(cols)], axis=1)
    linv = invs[0]
    for i in range(1, nb):
        lo, hi = i * b, (i + 1) * b
        row = -jnp.dot(invs[i], jnp.dot(lower[lo:hi, :lo], linv, precision=HIGH), precision=HIGH)
        top = jnp.pad(linv, ((0, 0), (0, b)))
        bottom = jnp.concatenate([row, invs[i]], axis=1)
        linv = jnp.concatenate([top, bottom], axis=0)
    return lower, linv


def shards(panel_rows, diag_blocks, adjoint, fill):
    n_col = lax.axis_size("col")
    n_pan = lax.axis_size("panel")
    c = lax.axis_index("col")
    p = lax.axis_index("panel")
    piece, width = panel_rows.shape

    flat = n_pan * n_col
    perm = [((dst % n_col) * n_pan + dst // n_col, dst) for dst in range(flat)]
    mine = lax.ppermute(panel_rows, ("panel", "col"), perm)
    col_rows = lax.all_gather(mine, "panel", axis=0, tiled=True)

    marks = fill.astype(BF16)
    col_blocks = fill.shape[1]
    per = piece // B

    def product(k):
        rows = lax.dynamic_slice_in_dim(adjoint, k * piece, piece, 0)
        m = lax.dynamic_slice_in_dim(marks, k * per, per, 0)
        masked = (rows.reshape(per, B, col_blocks, B) * m[:, None, :, None]).reshape(piece, -1)
        return jnp.dot(masked, col_rows, preferred_element_type=F32)

    parts = [product((c + s) % n_col) for s in range(n_col)]
    total = parts[0]
    for s in range(1, n_col):
        total = total + shift(parts[s], "col", n_col, s)
    moment = jnp.dot(total.T, panel_rows.astype(F32), precision=HIGH)
    stages = [("panel", n_pan, p, 1)]
    stages += [("col", n_col, c, 1 << k) for k in range(n_col.bit_length() - 1)]
    stages += [("panel", n_pan, p, 1 << k) for k in range(1, n_pan.bit_length() - 1)]
    moment = halving_sum(moment, stages)

    lower, linv = factor_and_inverse(diag_blocks, parts, 1)
    minv = jnp.dot(linv.T, linv, precision=HIGH)
    grad_panel = -jnp.dot(total, minv, precision=HIGH)
    grad_lower = jnp.tril(jnp.dot(jnp.dot(minv, moment, precision=HIGH), linv.T, precision=HIGH))

    eye = jnp.eye(width, dtype=F32)
    diag = jnp.sum(lower * eye, axis=0)
    half = 1.0 - 0.5 * eye

    def pullback(bar):
        inner = jnp.tril(jnp.dot(lower.T, bar, precision=HIGH)) * half
        sigma = jnp.dot(jnp.dot(linv.T, inner, precision=HIGH), linv, precision=HIGH)
        return 0.5 * (sigma + sigma.T)

    grad_diag = pullback(grad_lower) + pullback(eye * (2.0 / diag)[None, :])
    return (grad_panel, grad_diag)


def solution(mesh):
    in_specs = (P(("panel", "col"), None), P(), P("panel", "col"), P("panel", "col"))
    out_specs = (P(("panel", "col"), None), P())
    return jax.shard_map(shards, mesh=mesh, in_specs=in_specs, out_specs=out_specs, check_vma=False)
```
